32 devices in a mesh: pw: 8 (over z, y), band: 4 (over x, core).
Axes of the slice: x: 2, y: 2, z: 4, core: 2. Of those that a mesh axis runs over, the one named last changes fastest.
Arguments:
- psi_block: float32 [2, 8, 256, 128], P(None, 'band', 'pw'), may hold values from -6 to 6
- psi_all: bfloat16 [2, 1024, 256, 128], P(None, 'band', 'pw'), may hold values from -0.0234375 to 0.0234375
- potential: float32 [128, 128, 128], P('pw'), may hold values from -8 to 8
- stick_col: int32 [256], replicated, may hold values from 0 to 16383, as said below
Outputs:
- intersection: float32 [2, 8, 1024], P(None, 'pw', 'band')
- hpsi: float32 [2, 8, 256, 128], P(None, 'band', 'pw')
The draws below stay inside these ranges and needn't reach their ends.
Inputs may be any that keep to these rules, and one draw needn't show every extreme that they name: `stick_col`: distinct columns of the 128 x 128 plane; column 0 and column 16383 are always among them.
All inputs are finite; a program needn't handle non-finite values.
Results may differ from the reference program's by a relative error of at most 0.0029.
Values may be sent and summed in bfloat16 or wider, within the bound.
No kernel may reach another device: no remote copies, remote signals or barrier semaphores. Data moves between devices by JAX's collectives and lax.ppermute only.
A program may use at most 64 MiB of HBM per device.

```python
import jax
import jax.numpy as jnp
from jax import lax

NG = 128
ALLB_DEV = 256
STICKS = 256
PW = 32768
ALLB = 1024
NCOL = 8


def draw_stick_col(key, part):
    inner = jax.random.permutation(key, NG * NG - 2)[:STICKS - 2] + 1
    first = jnp.zeros((1,), jnp.int32)
    final = jnp.full((1,), NG * NG - 1, jnp.int32)
    return jnp.concatenate([first, inner.astype(jnp.int32), final])


def with_spikes(result, key, source, target, blocks, factor):
    def block_of(dim):
        return (jnp.arange(result.shape[dim]) // (result.shape[dim] // blocks)).reshape((-1,) + (1,) * (result.ndim - 1 - dim))

    one_side = jax.random.permutation(key, blocks)[block_of(target)]
    second = (block_of(target) + blocks // 2) % blocks
    return jnp.where((block_of(source) == one_side) | (block_of(source) == second), factor * result, result)


def level_of(key, dims, pieces, smallest, largest):
    def one(axis_at, shards_of):
        draws = jax.random.uniform(jax.random.fold_in(jax.random.fold_in(key, 6), axis_at), (shards_of,), jnp.float32, smallest / len(pieces), largest / len(pieces))
        return jnp.repeat(jnp.exp(draws), dims[axis_at] // shards_of).reshape((-1,) + (1,) * (len(dims) - axis_at - 1))

    factor_of = one(*pieces[0])
    for cut in pieces[1:]:
        factor_of = factor_of * one(*cut)
    return factor_of


def scatter_about(rng, dims, scale, reach, shards=(), kind=jnp.bfloat16):
    array = jax.random.normal(rng, dims, jnp.float32) * scale
    if len(shards) > 0:
        array = level_of(rng, dims, shards, -0.22, 0.18) * array
    return jnp.clip(array, min=-reach, max=reach).astype(kind)


def heavy_noise(rng, dims, spread, reach, split, heavy, held_as=jnp.bfloat16):
    values = spread * jax.random.normal(rng, dims, jnp.float32)
    if split:
        values = values * level_of(rng, dims, split, -0.22, 0.18)
    return jnp.clip(with_spikes(values, jax.random.fold_in(rng, 3), *heavy), -reach, reach).astype(held_as)


def setup_inputs(seed: int = 0) -> dict:
    arg_keys = jax.random.split(jax.random.key(seed), 5)
    return {
        "psi_block": heavy_noise(arg_keys[0], (2, NCOL, STICKS, NG), 1.0, 6.0, ((1, 4), (2, 8)), (2, 1, 8, 2.0), jnp.float32),
        "psi_all": scatter_about(arg_keys[1], (2, ALLB, STICKS, NG), (2 * PW) ** -0.5, 0.0234375, ((1, 4), (2, 8))),
        "potential": scatter_about(arg_keys[2], (NG, NG, NG), 2.0, 8.0, ((0, 8),), jnp.float32),
        "stick_col": draw_stick_col(jax.random.fold_in(arg_keys[4], 71), 0),
    }


def frequency(index, size):
    return jnp.where(index < size // 2, index, index - size)


def kinetic_table(stick_col):
    col_x = frequency(stick_col // NG, NG).astype(jnp.float32)
    col_y = frequency(stick_col % NG, NG).astype(jnp.float32)
    along = frequency(jnp.arange(NG, dtype=jnp.int32), NG).astype(jnp.float32)
    plane = col_x * col_x + col_y * col_y
    return 4.0 * (plane[:, None] + along[None, :] * along[None, :]) / float(NG * NG)


def apply_hamiltonian(coeffs, potential, stick_col, kinetic):
    real_full = jnp.zeros((NG, NG * NG), jnp.float32).at[:, stick_col].set(coeffs[0].T).reshape(NG, NG, NG)
    imag_full = jnp.zeros((NG, NG * NG), jnp.float32).at[:, stick_col].set(coeffs[1].T).reshape(NG, NG, NG)
    wave = jnp.fft.ifftn(lax.complex(real_full, imag_full))
    spectrum = jnp.fft.fftn(potential * wave).reshape(NG, NG * NG)[:, stick_col].T
    return jnp.stack([kinetic * coeffs[0] + jnp.real(spectrum), kinetic * coeffs[1] + jnp.imag(spectrum)])


def reference(psi_block, psi_all, potential, stick_col):
    kinetic = kinetic_table(stick_col)
    per_band = lax.map(lambda coeffs: apply_hamiltonian(coeffs, potential, stick_col, kinetic), jnp.moveaxis(psi_block, 1, 0))
    hpsi = jnp.moveaxis(per_band, 0, 1)
    rounded = lax.optimization_barrier(hpsi.astype(jnp.bfloat16)).astype(jnp.float32)
    flat_h = rounded.reshape(2, NCOL, PW)

    def product(left, right):
        return jnp.dot(left, right.T, precision=lax.Precision.HIGHEST, preferred_element_type=jnp.float32)

    def one_block(block_index):
        begin = (block_index * ALLB_DEV).astype(jnp.int32)
        block = lax.dynamic_slice_in_dim(psi_all, begin, ALLB_DEV, 1).astype(jnp.float32).reshape(2, ALLB_DEV, PW)
        real_part = product(flat_h[0], block[0]) + product(flat_h[1], block[1])
        imag_part = product(flat_h[0], block[1]) - product(flat_h[1], block[0])
        return jnp.stack([real_part, imag_part])

    blocks = lax.map(one_block, jnp.arange(ALLB // ALLB_DEV, dtype=jnp.int32))
    intersection = jnp.transpose(blocks, (1, 2, 0, 3)).reshape(2, NCOL, ALLB)
    return intersection, hpsi
```

```python
import math

import jax
import jax.numpy as jnp
from jax import lax
from jax.sharding import PartitionSpec as P


def frequency(index, size):
    return jnp.where(index < size // 2, index, index - size)


def kinetic_table(columns, grid_size):
    col_x = frequency(columns // grid_size, grid_size).astype(jnp.float32)
    col_y = frequency(columns % grid_size, grid_size).astype(jnp.float32)
    along = frequency(jnp.arange(grid_size, dtype=jnp.int32), grid_size).astype(jnp.float32)
    plane = col_x * col_x + col_y * col_y
    return 4.0 * (plane[:, None] + along[None, :] * along[None, :]) / float(grid_size * grid_size)


def dft_table(grid_size, sign):
    indices = jnp.arange(grid_size, dtype=jnp.int32)
    products = indices[:, None] * indices[None, :] % grid_size
    angles = 2.0 * math.pi / grid_size * products.astype(jnp.float32)
    cosine = jnp.cos(angles)
    sine = sign * jnp.sin(angles)
    return jnp.stack([jnp.stack([cosine, -sine]), jnp.stack([sine, cosine])])


def per_device(psi_block, psi_all, potential, stick_col):
    local_bands = psi_block.shape[1]
    sticks_dev = psi_block.shape[2]
    grid_size = psi_block.shape[3]
    fast = lax.Precision.HIGH
    rank = lax.axis_index("pw")
    pw_count = lax.axis_size("pw")
    my_columns = lax.dynamic_slice_in_dim(stick_col, rank * sticks_dev, sticks_dev)
    kinetic = kinetic_table(my_columns, grid_size)
    inverse = dft_table(grid_size, 1.0)
    forward = dft_table(grid_size, -1.0)
    cosine = inverse[0, 0]
    sine = inverse[1, 0]
    grid_iota = jnp.arange(grid_size, dtype=jnp.int32)
    col_x = stick_col // grid_size
    col_y = stick_col % grid_size
    phase_angles = (
        2.0
        * math.pi
        / grid_size
        * (grid_iota[:, None] * col_y[None, :] % grid_size).astype(jnp.float32)
    )
    phase_cos = jnp.cos(phase_angles)
    phase_sin = jnp.sin(phase_angles)
    place_rows = (col_x[:, None] == grid_iota[None, :]).astype(jnp.float32)
    pick_rows = (grid_iota[:, None] == col_x[None, :]).astype(jnp.float32)
    turned_pot = (jnp.transpose(potential, (0, 2, 1)) / float(grid_size**3))[None]

    def mult(left, right):
        return jnp.dot(left, right, precision=fast, preferred_element_type=jnp.float32)

    z_lines = jnp.einsum("dcvu,cbsu->bvds", inverse, psi_block, precision=fast)
    planes_in = lax.all_to_all(z_lines, "pw", split_axis=1, concat_axis=3, tiled=True)
    val_re = planes_in[:, :, 0, None, :]
    val_im = planes_in[:, :, 1, None, :]
    spread_re = val_re * phase_cos - val_im * phase_sin
    spread_im = val_re * phase_sin + val_im * phase_cos
    rows_re = mult(spread_re, place_rows)
    rows_im = mult(spread_im, place_rows)
    wave_re = (mult(rows_re, cosine) - mult(rows_im, sine)) * turned_pot
    wave_im = (mult(rows_re, sine) + mult(rows_im, cosine)) * turned_pot
    back_re = mult(wave_re, cosine) + mult(wave_im, sine)
    back_im = mult(wave_im, cosine) - mult(wave_re, sine)
    sel_re = mult(back_re, pick_rows)
    sel_im = mult(back_im, pick_rows)
    picked_re = jnp.sum(sel_re * phase_cos + sel_im * phase_sin, axis=2)
    picked_im = jnp.sum(sel_im * phase_cos - sel_re * phase_sin, axis=2)
    picked = jnp.stack([picked_re, picked_im], axis=2)
    sticks_back = lax.all_to_all(picked, "pw", split_axis=3, concat_axis=1, tiled=True)
    vpsi = jnp.einsum("dcvu,bucs->dbsv", forward, sticks_back, precision=fast)
    applied = kinetic[None, None] * psi_block + vpsi
    lowered = applied.astype(jnp.bfloat16)
    gathered = lax.all_gather(lowered, "band", axis=1, tiled=True)
    dims = (((1, 2), (1, 2)), ((), ()))

    def inner(left, right):
        return lax.dot_general(left, right, dims, preferred_element_type=jnp.float32)

    real_part = inner(gathered[0], psi_all[0]) + inner(gathered[1], psi_all[1])
    imag_part = inner(gathered[0], psi_all[1]) - inner(gathered[1], psi_all[0])
    partial_value = jnp.stack([real_part, imag_part])
    rows_dev = partial_value.shape[1] // pw_count
    pieces = partial_value.reshape(2, pw_count, rows_dev, partial_value.shape[-1])
    pieces = lax.all_to_all(pieces, "pw", split_axis=1, concat_axis=1, tiled=True)
    intersection = jnp.sum(pieces, axis=1)
    return (intersection, applied)


def solution(mesh):
    return jax.shard_map(
        per_device,
        mesh=mesh,
        in_specs=(
            P(None, "band", "pw", None),
            P(None, "band", "pw", None),
            P("pw", None, None),
            P(),
        ),
        out_specs=(P(None, "pw", "band"), P(None, "band", "pw", None)),
        check_vma=False,
    )
```

```python
import math

import jax
import jax.numpy as jnp
from jax import lax
from jax.sharding import PartitionSpec as P


def frequency(index, size):
    return jnp.where(index < size // 2, index, index - size)


def kinetic_table(columns, grid_size):
    col_x = frequency(columns // grid_size, grid_size).astype(jnp.float32)
    col_y = frequency(columns % grid_size, grid_size).astype(jnp.float32)
    along = frequency(jnp.arange(grid_size, dtype=jnp.int32), grid_size).astype(jnp.float32)
    plane = col_x * col_x + col_y * col_y
    return 4.0 * (plane[:, None] + along[None, :] * along[None, :]) / float(grid_size * grid_size)


def dft_table(grid_size, sign):
    indices = jnp.arange(grid_size, dtype=jnp.int32)
    products = indices[:, None] * indices[None, :] % grid_size
    angles = 2.0 * math.pi / grid_size * products.astype(jnp.float32)
    cosine = jnp.cos(angles)
    sine = sign * jnp.sin(angles)
    return jnp.stack([jnp.stack([cosine, -sine]), jnp.stack([sine, cosine])])


def per_device(psi_block, psi_all, potential, stick_col):
    sticks_dev = psi_block.shape[2]
    grid_size = psi_block.shape[3]
    fast = lax.Precision.HIGH
    rank = lax.axis_index("pw")
    pw_count = lax.axis_size("pw")
    planes = potential.shape[0]
    my_columns = lax.dynamic_slice_in_dim(stick_col, rank * sticks_dev, sticks_dev)
    kinetic = kinetic_table(my_columns, grid_size)
    inverse = dft_table(grid_size, 1.0)
    forward = dft_table(grid_size, -1.0)
    cosine = inverse[0, 0]
    sine = inverse[1, 0]
    grid_iota = jnp.arange(grid_size, dtype=jnp.int32)
    col_x = stick_col // grid_size
    col_y = stick_col % grid_size
    phase_angles = (
        2.0
        * math.pi
        / grid_size
        * (grid_iota[:, None] * col_x[None, :] % grid_size).astype(jnp.float32)
    )
    phase_cos = jnp.cos(phase_angles)
    phase_sin = jnp.sin(phase_angles)
    place_cols = (col_y[:, None] == grid_iota[None, :]).astype(jnp.float32)
    pick_cols = (grid_iota[:, None] == col_y[None, :]).astype(jnp.float32)
    scaled_pot = (potential / float(grid_size**3))[None]

    def mult(left, right):
        return jnp.dot(left, right, precision=fast, preferred_element_type=jnp.float32)

    z_lines = jnp.einsum("dczk,cbsk->zdbs", inverse, psi_block, precision=fast)
    received = lax.all_to_all(z_lines, "pw", split_axis=0, concat_axis=0, tiled=True)
    lanes = received.shape[1:]
    received = received.reshape((pw_count, planes) + lanes)
    amp = jnp.transpose(received, (2, 3, 1, 0, 4)).reshape(
        lanes[0], lanes[1], planes, pw_count * sticks_dev
    )
    val_re = amp[0][:, :, None, :]
    val_im = amp[1][:, :, None, :]
    spread_re = val_re * phase_cos - val_im * phase_sin
    spread_im = val_re * phase_sin + val_im * phase_cos
    rows_re = mult(spread_re, place_cols)
    rows_im = mult(spread_im, place_cols)
    wave_re = (mult(rows_re, cosine) - mult(rows_im, sine)) * scaled_pot
    wave_im = (mult(rows_re, sine) + mult(rows_im, cosine)) * scaled_pot
    back_re = mult(wave_re, cosine) + mult(wave_im, sine)
    back_im = mult(wave_im, cosine) - mult(wave_re, sine)
    sel_re = mult(back_re, pick_cols)
    sel_im = mult(back_im, pick_cols)
    picked_re = jnp.sum(sel_re * phase_cos + sel_im * phase_sin, axis=2)
    picked_im = jnp.sum(sel_im * phase_cos - sel_re * phase_sin, axis=2)
    picked = jnp.stack([picked_re, picked_im])
    outgoing = picked.reshape(lanes[0], lanes[1], planes, pw_count, sticks_dev)
    outgoing = jnp.transpose(outgoing, (3, 2, 0, 1, 4)).reshape((pw_count * planes,) + lanes)
    sticks_back = lax.all_to_all(outgoing, "pw", split_axis=0, concat_axis=0, tiled=True)
    vpsi = jnp.einsum("dckz,zcbs->dbsk", forward, sticks_back, precision=fast)
    applied = kinetic[None, None] * psi_block + vpsi
    lowered = applied.astype(jnp.bfloat16)
    gathered = lax.all_gather(lowered, "band", axis=1, tiled=True)
    turned = jnp.stack([-gathered[1], gathered[0]])
    both = jnp.concatenate([gathered, turned], axis=1)
    dims = (((0, 2, 3), (0, 2, 3)), ((), ()))
    partial_value = lax.dot_general(both, psi_all, dims, preferred_element_type=jnp.float32)
    partial_value = partial_value.reshape(2, gathered.shape[1], partial_value.shape[-1])
    rows_dev = partial_value.shape[1] // pw_count
    pieces = partial_value.reshape(2, pw_count, rows_dev, partial_value.shape[-1])
    pieces = lax.all_to_all(pieces, "pw", split_axis=1, concat_axis=1, tiled=True)
    intersection = jnp.sum(pieces, axis=1)
    return (intersection, applied)


def solution(mesh):
    return jax.shard_map(
        per_device,
        mesh=mesh,
        in_specs=(
            P(None, "band", "pw", None),
            P(None, "band", "pw", None),
            P("pw", None, None),
            P(),
        ),
        out_specs=(P(None, "pw", "band"), P(None, "band", "pw", None)),
        check_vma=False,
    )
```

```python
import math

import jax
import jax.numpy as jnp
from jax import lax
from jax.sharding import PartitionSpec as P


def frequency(index, size):
    return jnp.where(index < size // 2, index, index - size)


def kinetic_table(columns, grid_size):
    col_x = frequency(columns // grid_size, grid_size).astype(jnp.float32)
    col_y = frequency(columns % grid_size, grid_size).astype(jnp.float32)
    along = frequency(jnp.arange(grid_size, dtype=jnp.int32), grid_size).astype(jnp.float32)
    plane = col_x * col_x + col_y * col_y
    return 4.0 * (plane[:, None] + along[None, :] * along[None, :]) / float(grid_size * grid_size)


def dft_table(grid_size, sign):
    indices = jnp.arange(grid_size, dtype=jnp.int32)
    products = indices[:, None] * indices[None, :] % grid_size
    angles = 2.0 * math.pi / grid_size * products.astype(jnp.float32)
    cosine = jnp.cos(angles)
    sine = sign * jnp.sin(angles)
    return jnp.stack([jnp.stack([cosine, -sine]), jnp.stack([sine, cosine])])


def plane_tables(stick_col, grid_size):
    grid_iota = jnp.arange(grid_size, dtype=jnp.int32)
    col_x = stick_col // grid_size
    col_y = stick_col % grid_size
    phase_angles = (
        2.0
        * math.pi
        / grid_size
        * (grid_iota[:, None] * col_x[None, :] % grid_size).astype(jnp.float32)
    )
    place_cols = (col_y[:, None] == grid_iota[None, :]).astype(jnp.float32)
    pick_cols = (grid_iota[:, None] == col_y[None, :]).astype(jnp.float32)
    return jnp.cos(phase_angles), jnp.sin(phase_angles), place_cols, pick_cols


def mult(left, right):
    return jnp.dot(left, right, precision=lax.Precision.HIGH, preferred_element_type=jnp.float32)


def plane_phase(amp, pot, tables, grid_size):
    phase_cos, phase_sin, place_cols, pick_cols = tables
    inverse = dft_table(grid_size, 1.0)
    cosine = inverse[0, 0]
    sine = inverse[1, 0]
    scaled_pot = (pot / float(grid_size**3))[None]
    val_re = amp[0][:, :, None, :]
    val_im = amp[1][:, :, None, :]
    spread_re = val_re * phase_cos - val_im * phase_sin
    spread_im = val_re * phase_sin + val_im * phase_cos
    rows_re = mult(spread_re, place_cols)
    rows_im = mult(spread_im, place_cols)
    wave_re = (mult(rows_re, cosine) - mult(rows_im, sine)) * scaled_pot
    wave_im = (mult(rows_re, sine) + mult(rows_im, cosine)) * scaled_pot
    back_re = mult(wave_re, cosine) + mult(wave_im, sine)
    back_im = mult(wave_im, cosine) - mult(wave_re, sine)
    sel_re = mult(back_re, pick_cols)
    sel_im = mult(back_im, pick_cols)
    picked_re = jnp.sum(sel_re * phase_cos + sel_im * phase_sin, axis=2)
    picked_im = jnp.sum(sel_im * phase_cos - sel_re * phase_sin, axis=2)
    return jnp.stack([picked_re, picked_im])


def intersect(lowered, psi_all, pw_count):
    turned = jnp.stack([-lowered[1], lowered[0]])
    both = jnp.concatenate([lowered, turned], axis=1)
    dims = (((0, 2, 3), (0, 2, 3)), ((), ()))
    partial_value = lax.dot_general(both, psi_all, dims, preferred_element_type=jnp.float32)
    partial_value = partial_value.reshape(2, lowered.shape[1], partial_value.shape[-1])
    rows_dev = partial_value.shape[1] // pw_count
    pieces = partial_value.reshape(2, pw_count, rows_dev, partial_value.shape[-1])
    pieces = lax.all_to_all(pieces, "pw", split_axis=1, concat_axis=1, tiled=True)
    return jnp.sum(pieces, axis=1)


def per_device_spread(psi_block, psi_all, potential, stick_col):
    local_bands = psi_block.shape[1]
    sticks_dev = psi_block.shape[2]
    grid_size = psi_block.shape[3]
    fast = lax.Precision.HIGH
    rank = lax.axis_index("pw")
    band_rank = lax.axis_index("band")
    pw_count = lax.axis_size("pw")
    band_count = lax.axis_size("band")
    planes = potential.shape[0] // band_count
    all_bands = local_bands * band_count
    groups = pw_count * band_count
    my_columns = lax.dynamic_slice_in_dim(stick_col, rank * sticks_dev, sticks_dev)
    kinetic = kinetic_table(my_columns, grid_size)
    inverse = dft_table(grid_size, 1.0)
    forward = dft_table(grid_size, -1.0)
    tables = plane_tables(stick_col, grid_size)
    kin_part = kinetic[None, None] * psi_block / float(grid_size)
    sources = jnp.concatenate([psi_block, kin_part], axis=1)
    z_lines = jnp.einsum("dczk,cbsk->zdbs", inverse, sources, precision=fast)
    z_lines = z_lines.reshape((groups, planes) + z_lines.shape[1:])
    received = lax.all_to_all(z_lines, ("pw", "band"), split_axis=0, concat_axis=0, tiled=True)
    received = received.reshape(pw_count, band_count, planes, 2, 2, local_bands, sticks_dev)
    received = jnp.transpose(received, (4, 3, 1, 5, 2, 0, 6)).reshape(
        2, 2, all_bands, planes, pw_count * sticks_dev
    )
    pot = lax.dynamic_slice_in_dim(potential, band_rank * planes, planes)
    picked = plane_phase(received[0], pot, tables, grid_size) + received[1]
    outgoing = picked.reshape(2, all_bands, planes, pw_count, sticks_dev)
    outgoing = jnp.transpose(outgoing, (3, 2, 0, 1, 4))
    outgoing = jnp.broadcast_to(
        outgoing[:, None], (pw_count, band_count) + outgoing.shape[1:]
    ).reshape((groups,) + outgoing.shape[1:])
    gathered = lax.all_to_all(outgoing, ("pw", "band"), split_axis=0, concat_axis=0, tiled=True)
    gathered = gathered.reshape((groups * planes,) + gathered.shape[2:])
    hpsi = jnp.einsum("dckz,zcbs->dbsk", forward, gathered, precision=fast)
    applied = lax.dynamic_slice_in_dim(hpsi, band_rank * local_bands, local_bands, 1)
    intersection = intersect(hpsi.astype(jnp.bfloat16), psi_all, pw_count)
    return (intersection, applied)


def per_device_rows(psi_block, psi_all, potential, stick_col):
    sticks_dev = psi_block.shape[2]
    grid_size = psi_block.shape[3]
    fast = lax.Precision.HIGH
    rank = lax.axis_index("pw")
    pw_count = lax.axis_size("pw")
    planes = potential.shape[0]
    my_columns = lax.dynamic_slice_in_dim(stick_col, rank * sticks_dev, sticks_dev)
    kinetic = kinetic_table(my_columns, grid_size)
    inverse = dft_table(grid_size, 1.0)
    forward = dft_table(grid_size, -1.0)
    tables = plane_tables(stick_col, grid_size)
    z_lines = jnp.einsum("dczk,cbsk->zdbs", inverse, psi_block, precision=fast)
    received = lax.all_to_all(z_lines, "pw", split_axis=0, concat_axis=0, tiled=True)
    lanes = received.shape[1:]
    received = received.reshape((pw_count, planes) + lanes)
    amp = jnp.transpose(received, (2, 3, 1, 0, 4)).reshape(
        lanes[0], lanes[1], planes, pw_count * sticks_dev
    )
    picked = plane_phase(amp, potential, tables, grid_size)
    outgoing = picked.reshape(lanes[0], lanes[1], planes, pw_count, sticks_dev)
    outgoing = jnp.transpose(outgoing, (3, 2, 0, 1, 4)).reshape((pw_count * planes,) + lanes)
    sticks_back = lax.all_to_all(outgoing, "pw", split_axis=0, concat_axis=0, tiled=True)
    vpsi = jnp.einsum("dckz,zcbs->dbsk", forward, sticks_back, precision=fast)
    applied = kinetic[None, None] * psi_block + vpsi
    lowered = applied.astype(jnp.bfloat16)
    gathered = lax.all_gather(lowered, "band", axis=1, tiled=True)
    intersection = intersect(gathered, psi_all, pw_count)
    return (intersection, applied)


def per_device(psi_block, psi_all, potential, stick_col):
    band_count = lax.axis_size("band")
    if potential.shape[0] % band_count == 0:
        return per_device_spread(psi_block, psi_all, potential, stick_col)
    return per_device_rows(psi_block, psi_all, potential, stick_col)


def solution(mesh):
    return jax.shard_map(
        per_device,
        mesh=mesh,
        in_specs=(
            P(None, "band", "pw", None),
            P(None, "band", "pw", None),
            P("pw", None, None),
            P(),
        ),
        out_specs=(P(None, "pw", "band"), P(None, "band", "pw", None)),
        check_vma=False,
    )
```

```python
import math

import jax
import numpy as np
import jax.numpy as jnp
from jax import lax
from jax.sharding import PartitionSpec as P


def frequency(index, size):
    return jnp.where(index < size // 2, index, index - size)


def kinetic_table(columns, grid_size):
    col_x = frequency(columns // grid_size, grid_size).astype(jnp.float32)
    col_y = frequency(columns % grid_size, grid_size).astype(jnp.float32)
    along = frequency(jnp.arange(grid_size, dtype=jnp.int32), grid_size).astype(jnp.float32)
    plane = col_x * col_x + col_y * col_y
    return 4.0 * (plane[:, None] + along[None, :] * along[None, :]) / float(grid_size * grid_size)


def dft_table(grid_size, sign):
    indices = np.arange(grid_size)
    products = indices[:, None] * indices[None, :] % grid_size
    angles = 2.0 * np.pi / grid_size * products
    cosine = np.cos(angles)
    sine = sign * np.sin(angles)
    table = np.stack([np.stack([cosine, -sine]), np.stack([sine, cosine])])
    return jnp.asarray(table.astype(np.float32))


def plane_tables(stick_col, grid_size):
    grid_iota = jnp.arange(grid_size, dtype=jnp.int32)
    col_x = stick_col // grid_size
    col_y = stick_col % grid_size
    phase_angles = (
        2.0
        * math.pi
        / grid_size
        * (grid_iota[:, None] * col_x[None, :] % grid_size).astype(jnp.float32)
    )
    place_cols = (col_y[:, None] == grid_iota[None, :]).astype(jnp.float32)
    pick_cols = (grid_iota[:, None] == col_y[None, :]).astype(jnp.float32)
    return jnp.cos(phase_angles), jnp.sin(phase_angles), place_cols, pick_cols


def mult(left, right):
    return jnp.dot(left, right, precision=lax.Precision.HIGH, preferred_element_type=jnp.float32)


def plane_phase(amp, pot, tables, grid_size):
    phase_cos, phase_sin, place_cols, pick_cols = tables
    inverse = dft_table(grid_size, 1.0)
    cosine = inverse[0, 0]
    sine = inverse[1, 0]
    scaled_pot = (pot / float(grid_size**3))[None]
    val_re = amp[0][:, :, None, :]
    val_im = amp[1][:, :, None, :]
    spread_re = val_re * phase_cos - val_im * phase_sin
    spread_im = val_re * phase_sin + val_im * phase_cos
    rows_re = mult(spread_re, place_cols)
    rows_im = mult(spread_im, place_cols)
    wave_re = (mult(rows_re, cosine) - mult(rows_im, sine)) * scaled_pot
    wave_im = (mult(rows_re, sine) + mult(rows_im, cosine)) * scaled_pot
    back_re = mult(wave_re, cosine) + mult(wave_im, sine)
    back_im = mult(wave_im, cosine) - mult(wave_re, sine)
    sel_re = mult(back_re, pick_cols)
    sel_im = mult(back_im, pick_cols)
    picked_re = jnp.sum(sel_re * phase_cos + sel_im * phase_sin, axis=2)
    picked_im = jnp.sum(sel_im * phase_cos - sel_re * phase_sin, axis=2)
    return jnp.stack([picked_re, picked_im])


def intersect(lowered, psi_all, pw_count):
    turned = jnp.stack([-lowered[1], lowered[0]])
    both = jnp.concatenate([lowered, turned], axis=1)
    dims = (((2, 3), (2, 3)), ((0,), (0,)))
    partial_value = lax.dot_general(both, psi_all, dims, preferred_element_type=jnp.float32)
    partial_value = jnp.sum(partial_value, axis=0)
    partial_value = partial_value.reshape(2, lowered.shape[1], partial_value.shape[-1])
    rows_dev = partial_value.shape[1] // pw_count
    pieces = partial_value.reshape(2, pw_count, rows_dev, partial_value.shape[-1])
    pieces = lax.all_to_all(pieces, "pw", split_axis=1, concat_axis=1, tiled=True)
    return jnp.sum(pieces, axis=1)


def per_device_rows(psi_block, psi_all, potential, stick_col):
    sticks_dev = psi_block.shape[2]
    grid_size = psi_block.shape[3]
    fast = lax.Precision.HIGH
    rank = lax.axis_index("pw")
    pw_count = lax.axis_size("pw")
    planes = potential.shape[0]
    my_columns = lax.dynamic_slice_in_dim(stick_col, rank * sticks_dev, sticks_dev)
    kinetic = kinetic_table(my_columns, grid_size)
    inverse = dft_table(grid_size, 1.0)
    forward = dft_table(grid_size, -1.0)
    tables = plane_tables(stick_col, grid_size)
    z_lines = jnp.einsum("dczk,cbsk->zdbs", inverse, psi_block, precision=fast)
    received = lax.all_to_all(z_lines, "pw", split_axis=0, concat_axis=0, tiled=True)
    lanes = received.shape[1:]
    received = received.reshape((pw_count, planes) + lanes)
    amp = jnp.transpose(received, (2, 3, 1, 0, 4)).reshape(
        lanes[0], lanes[1], planes, pw_count * sticks_dev
    )
    picked = plane_phase(amp, potential, tables, grid_size)
    outgoing = picked.reshape(lanes[0], lanes[1], planes, pw_count, sticks_dev)
    outgoing = jnp.transpose(outgoing, (3, 2, 0, 1, 4)).reshape((pw_count * planes,) + lanes)
    sticks_back = lax.all_to_all(outgoing, "pw", split_axis=0, concat_axis=0, tiled=True)
    vpsi = jnp.einsum("dckz,zcbs->dbsk", forward, sticks_back, precision=fast)
    applied = kinetic[None, None] * psi_block + vpsi
    lowered = applied.astype(jnp.bfloat16)
    gathered = lax.all_gather(lowered, "band", axis=1, tiled=True)
    intersection = intersect(gathered, psi_all, pw_count)
    return (intersection, applied)


def per_device(psi_block, psi_all, potential, stick_col):
    return per_device_rows(psi_block, psi_all, potential, stick_col)


def solution(mesh):
    return jax.shard_map(
        per_device,
        mesh=mesh,
        in_specs=(
            P(None, "band", "pw", None),
            P(None, "band", "pw", None),
            P("pw", None, None),
            P(),
        ),
        out_specs=(P(None, "pw", "band"), P(None, "band", "pw", None)),
        check_vma=False,
    )
```

```python
import math

import jax
import numpy as np
import jax.numpy as jnp
from jax import lax
from jax.sharding import PartitionSpec as P
from jax.experimental import pallas as pl
from jax.experimental.pallas import tpu as pltpu


def frequency(index, size):
    return jnp.where(index < size // 2, index, index - size)


def kinetic_table(columns, grid_size):
    col_x = frequency(columns // grid_size, grid_size).astype(jnp.float32)
    col_y = frequency(columns % grid_size, grid_size).astype(jnp.float32)
    along = frequency(jnp.arange(grid_size, dtype=jnp.int32), grid_size).astype(jnp.float32)
    plane = col_x * col_x + col_y * col_y
    return 4.0 * (plane[:, None] + along[None, :] * along[None, :]) / float(grid_size * grid_size)


def dft_table(grid_size, sign):
    indices = np.arange(grid_size)
    products = indices[:, None] * indices[None, :] % grid_size
    angles = 2.0 * np.pi / grid_size * products
    cosine = np.cos(angles)
    sine = sign * np.sin(angles)
    table = np.stack([np.stack([cosine, -sine]), np.stack([sine, cosine])])
    return jnp.asarray(table.astype(np.float32))


def plane_tables(stick_col, grid_size):
    grid_iota = jnp.arange(grid_size, dtype=jnp.int32)
    col_x = stick_col // grid_size
    col_y = stick_col % grid_size
    phase_angles = (
        2.0
        * math.pi
        / grid_size
        * (grid_iota[:, None] * col_x[None, :] % grid_size).astype(jnp.float32)
    )
    place_cols = (col_y[:, None] == grid_iota[None, :]).astype(jnp.float32)
    pick_cols = (grid_iota[:, None] == col_y[None, :]).astype(jnp.float32)
    return jnp.cos(phase_angles), jnp.sin(phase_angles), place_cols, pick_cols


def mult(left, right):
    return jnp.dot(left, right, precision=lax.Precision.HIGH, preferred_element_type=jnp.float32)


def plane_phase(amp, pot, tables, grid_size):
    phase_cos, phase_sin, place_cols, pick_cols = tables
    inverse = dft_table(grid_size, 1.0)
    cosine = inverse[0, 0]
    sine = inverse[1, 0]
    scaled_pot = (pot / float(grid_size**3))[None]
    val_re = amp[0][:, :, None, :]
    val_im = amp[1][:, :, None, :]
    spread_re = val_re * phase_cos - val_im * phase_sin
    spread_im = val_re * phase_sin + val_im * phase_cos
    rows_re = mult(spread_re, place_cols)
    rows_im = mult(spread_im, place_cols)
    wave_re = (mult(rows_re, cosine) - mult(rows_im, sine)) * scaled_pot
    wave_im = (mult(rows_re, sine) + mult(rows_im, cosine)) * scaled_pot
    back_re = mult(wave_re, cosine) + mult(wave_im, sine)
    back_im = mult(wave_im, cosine) - mult(wave_re, sine)
    sel_re = mult(back_re, pick_cols)
    sel_im = mult(back_im, pick_cols)
    picked_re = jnp.sum(sel_re * phase_cos + sel_im * phase_sin, axis=2)
    picked_im = jnp.sum(sel_im * phase_cos - sel_re * phase_sin, axis=2)
    return jnp.stack([picked_re, picked_im])


def split_bf16(value):
    high = value.astype(jnp.bfloat16)
    low = (value - high.astype(jnp.float32)).astype(jnp.bfloat16)
    return high, low


def dot_f32(left, right):
    return jnp.dot(left, right, preferred_element_type=jnp.float32)


def exact_select(value, table):
    high, low = split_bf16(value)
    return dot_f32(high, table) + dot_f32(low, table)


def split_product(value, table_high, table_low):
    high, low = split_bf16(value)
    return dot_f32(high, table_high) + dot_f32(high, table_low) + dot_f32(low, table_high)


def plane_kernel(amp_ref, pot_ref, pcos_ref, psin_ref, place_ref, pick_ref, thigh_ref, tlow_ref, out_ref):
    count = amp_ref.shape[1]
    planes = pot_ref.shape[0]
    half = pcos_ref.shape[0]

    def body(i, carry):
        a_re = amp_ref[0, pl.ds(i, 1), :]
        a_im = amp_ref[1, pl.ds(i, 1), :]
        pc = pcos_ref[...]
        ps = psin_ref[...]
        spread = jnp.concatenate([a_re * pc - a_im * ps, a_re * ps + a_im * pc], axis=0)
        rows = exact_select(spread, place_ref[...])
        thigh = thigh_ref[...]
        tlow = tlow_ref[...]
        prod = split_product(rows, thigh, tlow)
        pot = pot_ref[i % planes]
        w_re = (prod[:half, :half] - prod[half:, half:]) * pot
        w_im = (prod[:half, half:] + prod[half:, :half]) * pot
        prod = split_product(jnp.concatenate([w_re, w_im], axis=0), thigh, tlow)
        b_re = prod[:half, :half] + prod[half:, half:]
        b_im = prod[half:, :half] - prod[:half, half:]
        sel = exact_select(jnp.concatenate([b_re, b_im], axis=0), pick_ref[...])
        s_re = sel[:half]
        s_im = sel[half:]
        out_ref[0, pl.ds(i, 1), :] = jnp.sum(s_re * pc + s_im * ps, axis=0, keepdims=True)
        out_ref[1, pl.ds(i, 1), :] = jnp.sum(s_im * pc - s_re * ps, axis=0, keepdims=True)
        return carry

    lax.fori_loop(0, count, body, 0)


def plane_phase_kernel(amp, pot, stick_col, grid_size):
    bands, planes, sticks = amp.shape[1:]
    phase_cos, phase_sin, place_cols, pick_cols = plane_tables(stick_col, grid_size)
    inverse = dft_table(grid_size, 1.0)
    table = jnp.concatenate([inverse[0, 0], inverse[1, 0]], axis=1)
    t_high, t_low = split_bf16(table)
    scaled_pot = pot / float(grid_size**3)
    flat = amp.reshape(2, bands * planes, sticks)
    vmem = pl.BlockSpec(memory_space=pltpu.VMEM)
    per_plane = 2 * (2 * 2 * grid_size * sticks * grid_size) + 2 * (3 * 2 * 2 * grid_size * grid_size * 2 * grid_size)
    out = pl.pallas_call(
        plane_kernel,
        out_shape=jax.ShapeDtypeStruct(flat.shape, jnp.float32),
        in_specs=[vmem] * 8,
        out_specs=vmem,
        cost_estimate=pl.CostEstimate(
            flops=per_plane * bands * planes,
            transcendentals=0,
            bytes_accessed=4 * (2 * flat.size + scaled_pot.size + 4 * grid_size * sticks),
        ),
    )(
        flat,
        scaled_pot,
        phase_cos,
        phase_sin,
        place_cols.astype(jnp.bfloat16),
        pick_cols.astype(jnp.bfloat16),
        t_high,
        t_low,
    )
    return out.reshape(2, bands, planes, sticks)


def intersect(lowered, psi_all, pw_count):
    turned = jnp.stack([-lowered[1], lowered[0]])
    both = jnp.concatenate([lowered, turned], axis=1)
    dims = (((2, 3), (2, 3)), ((0,), (0,)))
    partial_value = lax.dot_general(both, psi_all, dims, preferred_element_type=jnp.float32)
    partial_value = jnp.sum(partial_value, axis=0)
    partial_value = partial_value.reshape(2, lowered.shape[1], partial_value.shape[-1])
    rows_dev = partial_value.shape[1] // pw_count
    pieces = partial_value.reshape(2, pw_count, rows_dev, partial_value.shape[-1])
    pieces = lax.all_to_all(pieces, "pw", split_axis=1, concat_axis=1, tiled=True)
    return jnp.sum(pieces, axis=1)


def per_device_rows(psi_block, psi_all, potential, stick_col):
    sticks_dev = psi_block.shape[2]
    grid_size = psi_block.shape[3]
    fast = lax.Precision.HIGH
    rank = lax.axis_index("pw")
    pw_count = lax.axis_size("pw")
    planes = potential.shape[0]
    my_columns = lax.dynamic_slice_in_dim(stick_col, rank * sticks_dev, sticks_dev)
    kinetic = kinetic_table(my_columns, grid_size)
    inverse = dft_table(grid_size, 1.0)
    forward = dft_table(grid_size, -1.0)
    z_lines = jnp.einsum("dczk,cbsk->zdbs", inverse, psi_block, precision=fast)
    received = lax.all_to_all(z_lines, "pw", split_axis=0, concat_axis=0, tiled=True)
    lanes = received.shape[1:]
    received = received.reshape((pw_count, planes) + lanes)
    amp = jnp.transpose(received, (2, 3, 1, 0, 4)).reshape(
        lanes[0], lanes[1], planes, pw_count * sticks_dev
    )
    picked = plane_phase_kernel(amp, potential, stick_col, grid_size)
    outgoing = picked.reshape(lanes[0], lanes[1], planes, pw_count, sticks_dev)
    outgoing = jnp.transpose(outgoing, (3, 2, 0, 1, 4)).reshape((pw_count * planes,) + lanes)
    sticks_back = lax.all_to_all(outgoing, "pw", split_axis=0, concat_axis=0, tiled=True)
    vpsi = jnp.einsum("dckz,zcbs->dbsk", forward, sticks_back, precision=fast)
    applied = kinetic[None, None] * psi_block + vpsi
    lowered = applied.astype(jnp.bfloat16)
    gathered = lax.all_gather(lowered, "band", axis=1, tiled=True)
    intersection = intersect(gathered, psi_all, pw_count)
    return (intersection, applied)


def per_device(psi_block, psi_all, potential, stick_col):
    return per_device_rows(psi_block, psi_all, potential, stick_col)


def solution(mesh):
    return jax.shard_map(
        per_device,
        mesh=mesh,
        in_specs=(
            P(None, "band", "pw", None),
            P(None, "band", "pw", None),
            P("pw", None, None),
            P(),
        ),
        out_specs=(P(None, "pw", "band"), P(None, "band", "pw", None)),
        check_vma=False,
    )
```

```python
import math

import jax
import numpy as np
import jax.numpy as jnp
from jax import lax
from jax.sharding import PartitionSpec as P


def frequency(index, size):
    return jnp.where(index < size // 2, index, index - size)


def kinetic_table(columns, grid_size):
    col_x = frequency(columns // grid_size, grid_size).astype(jnp.float32)
    col_y = frequency(columns % grid_size, grid_size).astype(jnp.float32)
    along = frequency(jnp.arange(grid_size, dtype=jnp.int32), grid_size).astype(jnp.float32)
    plane = col_x * col_x + col_y * col_y
    return 4.0 * (plane[:, None] + along[None, :] * along[None, :]) / float(grid_size * grid_size)


def dft_table(grid_size, sign):
    indices = np.arange(grid_size)
    products = indices[:, None] * indices[None, :] % grid_size
    angles = 2.0 * np.pi / grid_size * products
    cosine = np.cos(angles)
    sine = sign * np.sin(angles)
    table = np.stack([np.stack([cosine, -sine]), np.stack([sine, cosine])])
    return jnp.asarray(table.astype(np.float32))


def plane_tables(stick_col, grid_size):
    grid_iota = jnp.arange(grid_size, dtype=jnp.int32)
    col_x = stick_col // grid_size
    col_y = stick_col % grid_size
    phase_angles = (
        2.0
        * math.pi
        / grid_size
        * (grid_iota[:, None] * col_x[None, :] % grid_size).astype(jnp.float32)
    )
    place_cols = (col_y[:, None] == grid_iota[None, :]).astype(jnp.float32)
    pick_cols = (grid_iota[:, None] == col_y[None, :]).astype(jnp.float32)
    return jnp.cos(phase_angles), jnp.sin(phase_angles), place_cols, pick_cols


def mult(left, right):
    return jnp.dot(left, right, precision=lax.Precision.HIGH, preferred_element_type=jnp.float32)


def plane_phase(amp, pot, tables, grid_size):
    phase_cos, phase_sin, place_cols, pick_cols = tables
    inverse = dft_table(grid_size, 1.0)
    cosine = inverse[0, 0]
    sine = inverse[1, 0]
    scaled_pot = (pot / float(grid_size**3))[None]
    val_re = amp[0][:, :, None, :]
    val_im = amp[1][:, :, None, :]
    spread_re = val_re * phase_cos - val_im * phase_sin
    spread_im = val_re * phase_sin + val_im * phase_cos
    rows_re = mult(spread_re, place_cols)
    rows_im = mult(spread_im, place_cols)
    shared = mult(rows_re + rows_im, cosine)
    wave_re = (shared - mult(rows_im, cosine + sine)) * scaled_pot
    wave_im = (shared + mult(rows_re, sine - cosine)) * scaled_pot
    shared = mult(wave_re + wave_im, cosine)
    back_re = shared - mult(wave_im, cosine - sine)
    back_im = shared - mult(wave_re, sine + cosine)
    sel_re = mult(back_re, pick_cols)
    sel_im = mult(back_im, pick_cols)
    picked_re = jnp.sum(sel_re * phase_cos + sel_im * phase_sin, axis=2)
    picked_im = jnp.sum(sel_im * phase_cos - sel_re * phase_sin, axis=2)
    return jnp.stack([picked_re, picked_im])


def intersect(lowered, psi_all, pw_count):
    turned = jnp.stack([-lowered[1], lowered[0]])
    both = jnp.concatenate([lowered, turned], axis=1)
    dims = (((2, 3), (2, 3)), ((0,), (0,)))
    partial_value = lax.dot_general(both, psi_all, dims, preferred_element_type=jnp.float32)
    partial_value = jnp.sum(partial_value, axis=0)
    partial_value = partial_value.reshape(2, lowered.shape[1], partial_value.shape[-1])
    rows_dev = partial_value.shape[1] // pw_count
    pieces = partial_value.reshape(2, pw_count, rows_dev, partial_value.shape[-1])
    pieces = lax.all_to_all(pieces, "pw", split_axis=1, concat_axis=1, tiled=True)
    return jnp.sum(pieces, axis=1)


def per_device_rows(psi_block, psi_all, potential, stick_col):
    sticks_dev = psi_block.shape[2]
    grid_size = psi_block.shape[3]
    fast = lax.Precision.HIGH
    rank = lax.axis_index("pw")
    pw_count = lax.axis_size("pw")
    planes = potential.shape[0]
    my_columns = lax.dynamic_slice_in_dim(stick_col, rank * sticks_dev, sticks_dev)
    kinetic = kinetic_table(my_columns, grid_size)
    inverse = dft_table(grid_size, 1.0)
    forward = dft_table(grid_size, -1.0)
    tables = plane_tables(stick_col, grid_size)
    z_lines = jnp.einsum("dczk,cbsk->zdbs", inverse, psi_block, precision=fast)
    received = lax.all_to_all(z_lines, "pw", split_axis=0, concat_axis=0, tiled=True)
    lanes = received.shape[1:]
    received = received.reshape((pw_count, planes) + lanes)
    amp = jnp.transpose(received, (2, 3, 1, 0, 4)).reshape(
        lanes[0], lanes[1], planes, pw_count * sticks_dev
    )
    picked = plane_phase(amp, potential, tables, grid_size)
    outgoing = picked.reshape(lanes[0], lanes[1], planes, pw_count, sticks_dev)
    outgoing = jnp.transpose(outgoing, (3, 2, 0, 1, 4)).reshape((pw_count * planes,) + lanes)
    sticks_back = lax.all_to_all(outgoing, "pw", split_axis=0, concat_axis=0, tiled=True)
    vpsi = jnp.einsum("dckz,zcbs->dbsk", forward, sticks_back, precision=fast)
    applied = kinetic[None, None] * psi_block + vpsi
    lowered = applied.astype(jnp.bfloat16)
    gathered = lax.all_gather(lowered, "band", axis=1, tiled=True)
    intersection = intersect(gathered, psi_all, pw_count)
    return (intersection, applied)


def per_device(psi_block, psi_all, potential, stick_col):
    return per_device_rows(psi_block, psi_all, potential, stick_col)


def solution(mesh):
    return jax.shard_map(
        per_device,
        mesh=mesh,
        in_specs=(
            P(None, "band", "pw", None),
            P(None, "band", "pw", None),
            P("pw", None, None),
            P(),
        ),
        out_specs=(P(None, "pw", "band"), P(None, "band", "pw", None)),
        check_vma=False,
    )
```

```python
import math

import jax
import numpy as np
import jax.numpy as jnp
from jax import lax
from jax.sharding import PartitionSpec as P


def frequency(index, size):
    return jnp.where(index < size // 2, index, index - size)


def kinetic_table(columns, grid_size):
    col_x = frequency(columns // grid_size, grid_size).astype(jnp.float32)
    col_y = frequency(columns % grid_size, grid_size).astype(jnp.float32)
    along = frequency(jnp.arange(grid_size, dtype=jnp.int32), grid_size).astype(jnp.float32)
    plane = col_x * col_x + col_y * col_y
    return 4.0 * (plane[:, None] + along[None, :] * along[None, :]) / float(grid_size * grid_size)


def dft_table(grid_size, sign):
    indices = np.arange(grid_size)
    products = indices[:, None] * indices[None, :] % grid_size
    angles = 2.0 * np.pi / grid_size * products
    cosine = np.cos(angles)
    sine = sign * np.sin(angles)
    table = np.stack([np.stack([cosine, -sine]), np.stack([sine, cosine])])
    return jnp.asarray(table.astype(np.float32))


def plane_tables(stick_col, grid_size):
    grid_iota = jnp.arange(grid_size, dtype=jnp.int32)
    col_x = stick_col // grid_size
    col_y = stick_col % grid_size
    phase_angles = (
        2.0
        * math.pi
        / grid_size
        * (grid_iota[:, None] * col_x[None, :] % grid_size).astype(jnp.float32)
    )
    place_cols = (col_y[:, None] == grid_iota[None, :]).astype(jnp.float32)
    pick_cols = (grid_iota[:, None] == col_y[None, :]).astype(jnp.float32)
    return jnp.cos(phase_angles), jnp.sin(phase_angles), place_cols, pick_cols


def mult(left, right):
    return jnp.dot(left, right, precision=lax.Precision.HIGH, preferred_element_type=jnp.float32)


def plane_phase(amp, pot, tables, grid_size):
    phase_cos, phase_sin, place_cols, pick_cols = tables
    inverse = dft_table(grid_size, 1.0)
    cosine = inverse[0, 0]
    sine = inverse[1, 0]
    scaled_pot = (pot / float(grid_size**3))[None]
    val_re = amp[0][:, :, None, :]
    val_im = amp[1][:, :, None, :]
    spread_re = val_re * phase_cos - val_im * phase_sin
    spread_im = val_re * phase_sin + val_im * phase_cos
    rows_re = mult(spread_re, place_cols)
    rows_im = mult(spread_im, place_cols)
    shared = mult(rows_re + rows_im, cosine)
    wave_re = (shared - mult(rows_im, cosine + sine)) * scaled_pot
    wave_im = (shared + mult(rows_re, sine - cosine)) * scaled_pot
    shared = mult(wave_re + wave_im, cosine)
    back_re = shared - mult(wave_im, cosine - sine)
    back_im = shared - mult(wave_re, sine + cosine)
    sel_re = mult(back_re, pick_cols)
    sel_im = mult(back_im, pick_cols)
    picked_re = jnp.sum(sel_re * phase_cos + sel_im * phase_sin, axis=2)
    picked_im = jnp.sum(sel_im * phase_cos - sel_re * phase_sin, axis=2)
    return jnp.stack([picked_re, picked_im])


def intersect(lowered, psi_all, pw_count):
    turned = jnp.stack([-lowered[1], lowered[0]])
    both = jnp.concatenate([lowered, turned], axis=1)
    dims = (((2, 3), (2, 3)), ((0,), (0,)))
    width = psi_all.shape[1] // 4
    partial_value = jnp.concatenate(
        [
            jnp.sum(
                lax.dot_general(
                    both,
                    psi_all[:, k * width : (k + 1) * width],
                    dims,
                    preferred_element_type=jnp.float32,
                ),
                axis=0,
            )
            for k in range(4)
        ],
        axis=-1,
    )
    partial_value = partial_value.reshape(2, lowered.shape[1], partial_value.shape[-1])
    rows_dev = partial_value.shape[1] // pw_count
    pieces = partial_value.reshape(2, pw_count, rows_dev, partial_value.shape[-1])
    pieces = lax.all_to_all(pieces, "pw", split_axis=1, concat_axis=1, tiled=True)
    return jnp.sum(pieces, axis=1)


def per_device_rows(psi_block, psi_all, potential, stick_col):
    sticks_dev = psi_block.shape[2]
    grid_size = psi_block.shape[3]
    fast = lax.Precision.HIGH
    rank = lax.axis_index("pw")
    pw_count = lax.axis_size("pw")
    planes = potential.shape[0]
    my_columns = lax.dynamic_slice_in_dim(stick_col, rank * sticks_dev, sticks_dev)
    kinetic = kinetic_table(my_columns, grid_size)
    inverse = dft_table(grid_size, 1.0)
    forward = dft_table(grid_size, -1.0)
    tables = plane_tables(stick_col, grid_size)
    z_lines = jnp.einsum("dczk,cbsk->zdbs", inverse, psi_block, precision=fast)
    received = lax.all_to_all(z_lines, "pw", split_axis=0, concat_axis=0, tiled=True)
    lanes = received.shape[1:]
    received = received.reshape((pw_count, planes) + lanes)
    amp = jnp.transpose(received, (2, 3, 1, 0, 4)).reshape(
        lanes[0], lanes[1], planes, pw_count * sticks_dev
    )
    picked = plane_phase(amp, potential, tables, grid_size)
    outgoing = picked.reshape(lanes[0], lanes[1], planes, pw_count, sticks_dev)
    outgoing = jnp.transpose(outgoing, (3, 2, 0, 1, 4)).reshape((pw_count * planes,) + lanes)
    sticks_back = lax.all_to_all(outgoing, "pw", split_axis=0, concat_axis=0, tiled=True)
    vpsi = jnp.einsum("dckz,zcbs->dbsk", forward, sticks_back, precision=fast)
    applied = kinetic[None, None] * psi_block + vpsi
    lowered = applied.astype(jnp.bfloat16)
    gathered = lax.all_gather(lowered, "band", axis=1, tiled=True)
    intersection = intersect(gathered, psi_all, pw_count)
    return (intersection, applied)


def per_device(psi_block, psi_all, potential, stick_col):
    return per_device_rows(psi_block, psi_all, potential, stick_col)


def solution(mesh):
    return jax.shard_map(
        per_device,
        mesh=mesh,
        in_specs=(
            P(None, "band", "pw", None),
            P(None, "band", "pw", None),
            P("pw", None, None),
            P(),
        ),
        out_specs=(P(None, "pw", "band"), P(None, "band", "pw", None)),
        check_vma=False,
    )
```

```python
import math

import jax
import numpy as np
import jax.numpy as jnp
from jax import lax
from jax.sharding import PartitionSpec as P


def frequency(index, size):
    return jnp.where(index < size // 2, index, index - size)


def kinetic_table(columns, grid_size):
    col_x = frequency(columns // grid_size, grid_size).astype(jnp.float32)
    col_y = frequency(columns % grid_size, grid_size).astype(jnp.float32)
    along = frequency(jnp.arange(grid_size, dtype=jnp.int32), grid_size).astype(jnp.float32)
    plane = col_x * col_x + col_y * col_y
    return 4.0 * (plane[:, None] + along[None, :] * along[None, :]) / float(grid_size * grid_size)


def dft_table(grid_size, sign):
    indices = np.arange(grid_size)
    products = indices[:, None] * indices[None, :] % grid_size
    angles = 2.0 * np.pi / grid_size * products
    cosine = np.cos(angles)
    sine = sign * np.sin(angles)
    table = np.stack([np.stack([cosine, -sine]), np.stack([sine, cosine])])
    return jnp.asarray(table.astype(np.float32))


def plane_tables(stick_col, grid_size):
    grid_iota = jnp.arange(grid_size, dtype=jnp.int32)
    col_x = stick_col // grid_size
    col_y = stick_col % grid_size
    phase_angles = (
        2.0
        * math.pi
        / grid_size
        * (grid_iota[:, None] * col_x[None, :] % grid_size).astype(jnp.float32)
    )
    place_cols = (col_y[:, None] == grid_iota[None, :]).astype(jnp.float32)
    pick_cols = (grid_iota[:, None] == col_y[None, :]).astype(jnp.float32)
    return jnp.cos(phase_angles), jnp.sin(phase_angles), place_cols, pick_cols


def mult(left, right):
    return jnp.dot(left, right, precision=lax.Precision.HIGH, preferred_element_type=jnp.float32)


def plane_phase(amp, pot, tables, grid_size):
    phase_cos, phase_sin, place_cols, pick_cols = tables
    inverse = dft_table(grid_size, 1.0)
    cosine = inverse[0, 0]
    sine = inverse[1, 0]
    scaled_pot = (pot / float(grid_size**3))[None]
    val_re = amp[0][:, :, None, :]
    val_im = amp[1][:, :, None, :]
    spread_re = val_re * phase_cos - val_im * phase_sin
    spread_im = val_re * phase_sin + val_im * phase_cos
    rows_re = mult(spread_re, place_cols)
    rows_im = mult(spread_im, place_cols)
    into_real = jnp.concatenate(
        [jnp.concatenate([cosine, sine], axis=1), jnp.concatenate([-sine, cosine], axis=1)], axis=0
    )
    into_spec = jnp.concatenate(
        [jnp.concatenate([cosine, -sine], axis=1), jnp.concatenate([sine, cosine], axis=1)], axis=0
    )
    wave = mult(jnp.concatenate([rows_re, rows_im], axis=-1), into_real)
    wave = (wave.reshape(wave.shape[:-1] + (2, grid_size)) * scaled_pot[..., None, :]).reshape(wave.shape)
    back = mult(wave, into_spec)
    back_re = back[..., :grid_size]
    back_im = back[..., grid_size:]
    sel_re = mult(back_re, pick_cols)
    sel_im = mult(back_im, pick_cols)
    picked_re = jnp.sum(sel_re * phase_cos + sel_im * phase_sin, axis=2)
    picked_im = jnp.sum(sel_im * phase_cos - sel_re * phase_sin, axis=2)
    return jnp.stack([picked_re, picked_im])


def intersect(lowered, psi_all, pw_count):
    turned = jnp.stack([-lowered[1], lowered[0]])
    both = jnp.concatenate([lowered, turned], axis=1)
    dims = (((2, 3), (2, 3)), ((0,), (0,)))
    width = psi_all.shape[1] // 4
    partial_value = jnp.concatenate(
        [
            jnp.sum(
                lax.dot_general(
                    both,
                    psi_all[:, k * width : (k + 1) * width],
                    dims,
                    preferred_element_type=jnp.float32,
                ),
                axis=0,
            )
            for k in range(4)
        ],
        axis=-1,
    )
    partial_value = partial_value.reshape(2, lowered.shape[1], partial_value.shape[-1])
    rows_dev = partial_value.shape[1] // pw_count
    pieces = partial_value.reshape(2, pw_count, rows_dev, partial_value.shape[-1])
    pieces = lax.all_to_all(pieces, "pw", split_axis=1, concat_axis=1, tiled=True)
    return jnp.sum(pieces, axis=1)


def per_device_rows(psi_block, psi_all, potential, stick_col):
    sticks_dev = psi_block.shape[2]
    grid_size = psi_block.shape[3]
    fast = lax.Precision.HIGH
    rank = lax.axis_index("pw")
    pw_count = lax.axis_size("pw")
    planes = potential.shape[0]
    my_columns = lax.dynamic_slice_in_dim(stick_col, rank * sticks_dev, sticks_dev)
    kinetic = kinetic_table(my_columns, grid_size)
    inverse = dft_table(grid_size, 1.0)
    forward = dft_table(grid_size, -1.0)
    tables = plane_tables(stick_col, grid_size)
    z_lines = jnp.einsum("dczk,cbsk->zdbs", inverse, psi_block, precision=fast)
    received = lax.all_to_all(z_lines, "pw", split_axis=0, concat_axis=0, tiled=True)
    lanes = received.shape[1:]
    received = received.reshape((pw_count, planes) + lanes)
    amp = jnp.transpose(received, (2, 3, 1, 0, 4)).reshape(
        lanes[0], lanes[1], planes, pw_count * sticks_dev
    )
    picked = plane_phase(amp, potential, tables, grid_size)
    outgoing = picked.reshape(lanes[0], lanes[1], planes, pw_count, sticks_dev)
    outgoing = jnp.transpose(outgoing, (3, 2, 0, 1, 4)).reshape((pw_count * planes,) + lanes)
    sticks_back = lax.all_to_all(outgoing, "pw", split_axis=0, concat_axis=0, tiled=True)
    vpsi = jnp.einsum("dckz,zcbs->dbsk", forward, sticks_back, precision=fast)
    applied = kinetic[None, None] * psi_block + vpsi
    lowered = applied.astype(jnp.bfloat16)
    gathered = lax.all_gather(lowered, "band", axis=1, tiled=True)
    intersection = intersect(gathered, psi_all, pw_count)
    return (intersection, applied)


def per_device(psi_block, psi_all, potential, stick_col):
    return per_device_rows(psi_block, psi_all, potential, stick_col)


def solution(mesh):
    return jax.shard_map(
        per_device,
        mesh=mesh,
        in_specs=(
            P(None, "band", "pw", None),
            P(None, "band", "pw", None),
            P("pw", None, None),
            P(),
        ),
        out_specs=(P(None, "pw", "band"), P(None, "band", "pw", None)),
        check_vma=False,
    )
```

```python
import math

import jax
import numpy as np
import jax.numpy as jnp
from jax import lax
from jax.sharding import PartitionSpec as P


def frequency(index, size):
    return jnp.where(index < size // 2, index, index - size)


def kinetic_table(columns, grid_size):
    col_x = frequency(columns // grid_size, grid_size).astype(jnp.float32)
    col_y = frequency(columns % grid_size, grid_size).astype(jnp.float32)
    along = frequency(jnp.arange(grid_size, dtype=jnp.int32), grid_size).astype(jnp.float32)
    plane = col_x * col_x + col_y * col_y
    return 4.0 * (plane[:, None] + along[None, :] * along[None, :]) / float(grid_size * grid_size)


def dft_table(grid_size, sign):
    indices = np.arange(grid_size)
    products = indices[:, None] * indices[None, :] % grid_size
    angles = 2.0 * np.pi / grid_size * products
    cosine = np.cos(angles)
    sine = sign * np.sin(angles)
    table = np.stack([np.stack([cosine, -sine]), np.stack([sine, cosine])])
    return jnp.asarray(table.astype(np.float32))


def plane_tables(stick_col, grid_size):
    grid_iota = jnp.arange(grid_size, dtype=jnp.int32)
    col_x = stick_col // grid_size
    col_y = stick_col % grid_size
    phase_angles = (
        2.0
        * math.pi
        / grid_size
        * (grid_iota[:, None] * col_x[None, :] % grid_size).astype(jnp.float32)
    )
    place_cols = (col_y[:, None] == grid_iota[None, :]).astype(jnp.float32)
    pick_cols = (grid_iota[:, None] == col_y[None, :]).astype(jnp.float32)
    return jnp.cos(phase_angles), jnp.sin(phase_angles), place_cols, pick_cols


def mult(left, right):
    return jnp.dot(left, right, precision=lax.Precision.HIGH, preferred_element_type=jnp.float32)


def plane_phase(amp, pot, tables, grid_size):
    phase_cos, phase_sin, place_cols, pick_cols = tables
    inverse = dft_table(grid_size, 1.0)
    cosine = inverse[0, 0]
    sine = inverse[1, 0]
    scaled_pot = (pot / float(grid_size**3))[None]
    val_re = amp[0][:, :, None, :]
    val_im = amp[1][:, :, None, :]
    spread_re = val_re * phase_cos - val_im * phase_sin
    spread_im = val_re * phase_sin + val_im * phase_cos
    rows_re = mult(spread_re, place_cols)
    rows_im = mult(spread_im, place_cols)
    shared = mult(rows_re + rows_im, cosine)
    wave_re = (shared - mult(rows_im, cosine + sine)) * scaled_pot
    wave_im = (shared + mult(rows_re, sine - cosine)) * scaled_pot
    shared = mult(wave_re + wave_im, cosine)
    back_re = shared - mult(wave_im, cosine - sine)
    back_im = shared - mult(wave_re, sine + cosine)
    sel_re = mult(back_re, pick_cols)
    sel_im = mult(back_im, pick_cols)
    picked_re = jnp.sum(sel_re * phase_cos + sel_im * phase_sin, axis=2)
    picked_im = jnp.sum(sel_im * phase_cos - sel_re * phase_sin, axis=2)
    return jnp.stack([picked_re, picked_im])


def intersect(lowered, psi_all, pw_count):
    turned = jnp.stack([-lowered[1], lowered[0]])
    both = jnp.concatenate([lowered, turned], axis=1)
    dims = (((1, 2), (1, 2)), ((), ()))
    partial_value = sum(
        lax.dot_general(both[part], psi_all[part], dims, preferred_element_type=jnp.float32)
        for part in range(psi_all.shape[0])
    )
    partial_value = partial_value.reshape(2, lowered.shape[1], partial_value.shape[-1])
    rows_dev = partial_value.shape[1] // pw_count
    pieces = partial_value.reshape(2, pw_count, rows_dev, partial_value.shape[-1])
    pieces = lax.all_to_all(pieces, "pw", split_axis=1, concat_axis=1, tiled=True)
    return jnp.sum(pieces, axis=1)


def per_device_rows(psi_block, psi_all, potential, stick_col):
    sticks_dev = psi_block.shape[2]
    grid_size = psi_block.shape[3]
    fast = lax.Precision.HIGH
    rank = lax.axis_index("pw")
    pw_count = lax.axis_size("pw")
    planes = potential.shape[0]
    my_columns = lax.dynamic_slice_in_dim(stick_col, rank * sticks_dev, sticks_dev)
    kinetic = kinetic_table(my_columns, grid_size)
    inverse = dft_table(grid_size, 1.0)
    forward = dft_table(grid_size, -1.0)
    tables = plane_tables(stick_col, grid_size)
    z_lines = jnp.einsum("dczk,cbsk->zdbs", inverse, psi_block, precision=fast)
    received = lax.all_to_all(z_lines, "pw", split_axis=0, concat_axis=0, tiled=True)
    lanes = received.shape[1:]
    received = received.reshape((pw_count, planes) + lanes)
    amp = jnp.transpose(received, (2, 3, 1, 0, 4)).reshape(
        lanes[0], lanes[1], planes, pw_count * sticks_dev
    )
    picked = plane_phase(amp, potential, tables, grid_size)
    outgoing = picked.reshape(lanes[0], lanes[1], planes, pw_count, sticks_dev)
    outgoing = jnp.transpose(outgoing, (3, 2, 0, 1, 4)).reshape((pw_count * planes,) + lanes)
    sticks_back = lax.all_to_all(outgoing, "pw", split_axis=0, concat_axis=0, tiled=True)
    vpsi = jnp.einsum("dckz,zcbs->dbsk", forward, sticks_back, precision=fast)
    applied = kinetic[None, None] * psi_block + vpsi
    lowered = applied.astype(jnp.bfloat16)
    gathered = lax.all_gather(lowered, "band", axis=1, tiled=True)
    intersection = intersect(gathered, psi_all, pw_count)
    return (intersection, applied)


def per_device(psi_block, psi_all, potential, stick_col):
    return per_device_rows(psi_block, psi_all, potential, stick_col)


def solution(mesh):
    return jax.shard_map(
        per_device,
        mesh=mesh,
        in_specs=(
            P(None, "band", "pw", None),
            P(None, "band", "pw", None),
            P("pw", None, None),
            P(),
        ),
        out_specs=(P(None, "pw", "band"), P(None, "band", "pw", None)),
        check_vma=False,
    )
```

```python
import math

import jax
import numpy as np
import jax.numpy as jnp
from jax import lax
from jax.sharding import PartitionSpec as P


def frequency(index, size):
    return jnp.where(index < size // 2, index, index - size)


def kinetic_table(columns, grid_size):
    col_x = frequency(columns // grid_size, grid_size).astype(jnp.float32)
    col_y = frequency(columns % grid_size, grid_size).astype(jnp.float32)
    along = frequency(jnp.arange(grid_size, dtype=jnp.int32), grid_size).astype(jnp.float32)
    plane = col_x * col_x + col_y * col_y
    return 4.0 * (plane[:, None] + along[None, :] * along[None, :]) / float(grid_size * grid_size)


def dft_table(grid_size, sign):
    indices = np.arange(grid_size)
    products = indices[:, None] * indices[None, :] % grid_size
    angles = 2.0 * np.pi / grid_size * products
    cosine = np.cos(angles)
    sine = sign * np.sin(angles)
    table = np.stack([np.stack([cosine, -sine]), np.stack([sine, cosine])])
    return jnp.asarray(table.astype(np.float32))


def plane_tables(stick_col, grid_size):
    grid_iota = jnp.arange(grid_size, dtype=jnp.int32)
    col_x = stick_col // grid_size
    col_y = stick_col % grid_size
    phase_angles = (
        2.0
        * math.pi
        / grid_size
        * (grid_iota[:, None] * col_x[None, :] % grid_size).astype(jnp.float32)
    )
    place_cols = (col_y[:, None] == grid_iota[None, :]).astype(jnp.float32)
    pick_cols = (grid_iota[:, None] == col_y[None, :]).astype(jnp.float32)
    return jnp.cos(phase_angles), jnp.sin(phase_angles), place_cols, pick_cols


def mult(left, right):
    return jnp.dot(left, right, precision=lax.Precision.HIGH, preferred_element_type=jnp.float32)


def plane_phase(amp, pot, tables, grid_size):
    phase_cos, phase_sin, place_cols, pick_cols = tables
    inverse = dft_table(grid_size, 1.0)
    cosine = inverse[0, 0]
    sine = inverse[1, 0]
    scaled_pot = (pot / float(grid_size**3))[None]
    val_re = amp[0][:, :, None, :]
    val_im = amp[1][:, :, None, :]
    spread_re = val_re * phase_cos - val_im * phase_sin
    spread_im = val_re * phase_sin + val_im * phase_cos
    rows_re = mult(spread_re, place_cols)
    rows_im = mult(spread_im, place_cols)
    shared = mult(rows_re + rows_im, cosine)
    wave_re = (shared - mult(rows_im, cosine + sine)) * scaled_pot
    wave_im = (shared + mult(rows_re, sine - cosine)) * scaled_pot
    shared = mult(wave_re + wave_im, cosine)
    back_re = shared - mult(wave_im, cosine - sine)
    back_im = shared - mult(wave_re, sine + cosine)
    sel_re = mult(back_re, pick_cols)
    sel_im = mult(back_im, pick_cols)
    picked_re = jnp.sum(sel_re * phase_cos + sel_im * phase_sin, axis=2)
    picked_im = jnp.sum(sel_im * phase_cos - sel_re * phase_sin, axis=2)
    return jnp.stack([picked_re, picked_im])


def intersect(lowered, psi_all, pw_count):
    turned = jnp.stack([-lowered[1], lowered[0]])
    both = jnp.concatenate([lowered, turned], axis=1)
    dims = (((2, 3), (2, 3)), ((0,), (0,)))
    width = psi_all.shape[1] // 4
    partial_value = jnp.concatenate(
        [
            jnp.sum(
                lax.dot_general(
                    both,
                    psi_all[:, k * width : (k + 1) * width],
                    dims,
                    preferred_element_type=jnp.float32,
                ),
                axis=0,
            )
            for k in range(4)
        ],
        axis=-1,
    )
    partial_value = partial_value.reshape(2, lowered.shape[1], partial_value.shape[-1])
    rows_dev = partial_value.shape[1] // pw_count
    pieces = partial_value.reshape(2, pw_count, rows_dev, partial_value.shape[-1])
    pieces = lax.all_to_all(pieces, "pw", split_axis=1, concat_axis=1, tiled=True)
    return jnp.sum(pieces, axis=1)


def per_device_rows(psi_block, psi_all, potential, stick_col):
    sticks_dev = psi_block.shape[2]
    grid_size = psi_block.shape[3]
    fast = lax.Precision.HIGH
    rank = lax.axis_index("pw")
    pw_count = lax.axis_size("pw")
    planes = potential.shape[0]
    my_columns = lax.dynamic_slice_in_dim(stick_col, rank * sticks_dev, sticks_dev)
    kinetic = kinetic_table(my_columns, grid_size)
    inverse = dft_table(grid_size, 1.0)
    forward = dft_table(grid_size, -1.0)
    tables = plane_tables(stick_col, grid_size)
    z_lines = jnp.einsum("dczk,cbsk->zdbs", inverse, psi_block, precision=fast)
    received = lax.all_to_all(z_lines, "pw", split_axis=0, concat_axis=0, tiled=True)
    lanes = received.shape[1:]
    received = received.reshape((pw_count, planes) + lanes)
    amp = jnp.transpose(received, (2, 3, 1, 0, 4)).reshape(
        lanes[0], lanes[1], planes, pw_count * sticks_dev
    )
    picked = plane_phase(amp, potential, tables, grid_size)
    outgoing = picked.reshape(lanes[0], lanes[1], planes, pw_count, sticks_dev)
    outgoing = jnp.transpose(outgoing, (3, 2, 0, 1, 4)).reshape((pw_count * planes,) + lanes)
    sticks_back = lax.all_to_all(outgoing, "pw", split_axis=0, concat_axis=0, tiled=True)
    vpsi = jnp.einsum("dckz,zcbs->dbsk", forward, sticks_back, precision=fast)
    applied = kinetic[None, None] * psi_block + vpsi
    lowered = applied.astype(jnp.bfloat16)
    gathered = lax.all_gather(lowered, "band", axis=1, tiled=True)
    psi_all, _ = lax.optimization_barrier((psi_all, outgoing))
    intersection = intersect(gathered, psi_all, pw_count)
    return (intersection, applied)


def per_device(psi_block, psi_all, potential, stick_col):
    return per_device_rows(psi_block, psi_all, potential, stick_col)


def solution(mesh):
    return jax.shard_map(
        per_device,
        mesh=mesh,
        in_specs=(
            P(None, "band", "pw", None),
            P(None, "band", "pw", None),
            P("pw", None, None),
            P(),
        ),
        out_specs=(P(None, "pw", "band"), P(None, "band", "pw", None)),
        check_vma=False,
    )
```

```python
import math

import jax
import numpy as np
import jax.numpy as jnp
from jax import lax
from jax.sharding import PartitionSpec as P


def frequency(index, size):
    return jnp.where(index < size // 2, index, index - size)


def kinetic_table(columns, grid_size):
    col_x = frequency(columns // grid_size, grid_size).astype(jnp.float32)
    col_y = frequency(columns % grid_size, grid_size).astype(jnp.float32)
    along = frequency(jnp.arange(grid_size, dtype=jnp.int32), grid_size).astype(jnp.float32)
    plane = col_x * col_x + col_y * col_y
    return 4.0 * (plane[:, None] + along[None, :] * along[None, :]) / float(grid_size * grid_size)


def dft_table(grid_size, sign):
    indices = np.arange(grid_size)
    products = indices[:, None] * indices[None, :] % grid_size
    angles = 2.0 * np.pi / grid_size * products
    cosine = np.cos(angles)
    sine = sign * np.sin(angles)
    table = np.stack([np.stack([cosine, -sine]), np.stack([sine, cosine])])
    return jnp.asarray(table.astype(np.float32))


def plane_tables(stick_col, grid_size):
    grid_iota = jnp.arange(grid_size, dtype=jnp.int32)
    col_x = stick_col // grid_size
    col_y = stick_col % grid_size
    phase_angles = (
        2.0
        * math.pi
        / grid_size
        * (grid_iota[:, None] * col_x[None, :] % grid_size).astype(jnp.float32)
    )
    place_cols = (col_y[:, None] == grid_iota[None, :]).astype(jnp.float32)
    pick_cols = (grid_iota[:, None] == col_y[None, :]).astype(jnp.float32)
    return jnp.cos(phase_angles), jnp.sin(phase_angles), place_cols, pick_cols


def mult(left, right):
    return jnp.dot(left, right, precision=lax.Precision.HIGH, preferred_element_type=jnp.float32)


def plane_phase(amp, pot, tables, grid_size):
    phase_cos, phase_sin, place_cols, pick_cols = tables
    inverse = dft_table(grid_size, 1.0)
    cosine = inverse[0, 0]
    sine = inverse[1, 0]
    scaled_pot = (pot / float(grid_size**3))[None]
    val_re = amp[0][:, :, None, :]
    val_im = amp[1][:, :, None, :]
    spread_re = val_re * phase_cos - val_im * phase_sin
    spread_im = val_re * phase_sin + val_im * phase_cos
    rows_re = mult(spread_re, place_cols)
    rows_im = mult(spread_im, place_cols)
    shared = mult(rows_re + rows_im, cosine)
    wave_re = (shared - mult(rows_im, cosine + sine)) * scaled_pot
    wave_im = (shared + mult(rows_re, sine - cosine)) * scaled_pot
    shared = mult(wave_re + wave_im, cosine)
    back_re = shared - mult(wave_im, cosine - sine)
    back_im = shared - mult(wave_re, sine + cosine)
    sel_re = mult(back_re, pick_cols)
    sel_im = mult(back_im, pick_cols)
    picked_re = jnp.sum(sel_re * phase_cos + sel_im * phase_sin, axis=2)
    picked_im = jnp.sum(sel_im * phase_cos - sel_re * phase_sin, axis=2)
    return jnp.stack([picked_re, picked_im])


def intersect(lowered, psi_all, pw_count):
    turned = jnp.stack([-lowered[1], lowered[0]])
    both = jnp.concatenate([lowered, turned], axis=1)
    dims = (((2, 3), (2, 3)), ((0,), (0,)))
    width = psi_all.shape[1] // 4
    partial_value = jnp.concatenate(
        [
            jnp.sum(
                lax.dot_general(
                    both,
                    psi_all[:, k * width : (k + 1) * width],
                    dims,
                    preferred_element_type=jnp.float32,
                ),
                axis=0,
            )
            for k in range(4)
        ],
        axis=-1,
    )
    partial_value = partial_value.reshape(2, lowered.shape[1], partial_value.shape[-1])
    rows_dev = partial_value.shape[1] // pw_count
    pieces = partial_value.reshape(2, pw_count, rows_dev, partial_value.shape[-1])
    pieces = lax.all_to_all(pieces, "pw", split_axis=1, concat_axis=1, tiled=True)
    return jnp.sum(pieces, axis=1)


def per_device_rows(psi_block, psi_all, potential, stick_col):
    sticks_dev = psi_block.shape[2]
    grid_size = psi_block.shape[3]
    fast = lax.Precision.HIGH
    rank = lax.axis_index("pw")
    pw_count = lax.axis_size("pw")
    planes = potential.shape[0]
    my_columns = lax.dynamic_slice_in_dim(stick_col, rank * sticks_dev, sticks_dev)
    kinetic = kinetic_table(my_columns, grid_size)
    inverse = dft_table(grid_size, 1.0)
    forward = dft_table(grid_size, -1.0)
    tables = plane_tables(stick_col, grid_size)
    z_lines = jnp.einsum("dczk,cbsk->zdbs", inverse, psi_block, precision=fast)
    received = lax.all_to_all(
        z_lines.astype(jnp.bfloat16), "pw", split_axis=0, concat_axis=0, tiled=True
    ).astype(jnp.float32)
    lanes = received.shape[1:]
    received = received.reshape((pw_count, planes) + lanes)
    amp = jnp.transpose(received, (2, 3, 1, 0, 4)).reshape(
        lanes[0], lanes[1], planes, pw_count * sticks_dev
    )
    picked = plane_phase(amp, potential, tables, grid_size)
    outgoing = picked.reshape(lanes[0], lanes[1], planes, pw_count, sticks_dev)
    outgoing = jnp.transpose(outgoing, (3, 2, 0, 1, 4)).reshape((pw_count * planes,) + lanes)
    sticks_back = lax.all_to_all(
        outgoing.astype(jnp.bfloat16), "pw", split_axis=0, concat_axis=0, tiled=True
    ).astype(jnp.float32)
    vpsi = jnp.einsum("dckz,zcbs->dbsk", forward, sticks_back, precision=fast)
    applied = kinetic[None, None] * psi_block + vpsi
    lowered = applied.astype(jnp.bfloat16)
    gathered = lax.all_gather(lowered, "band", axis=1, tiled=True)
    intersection = intersect(gathered, psi_all, pw_count)
    return (intersection, applied)


def per_device(psi_block, psi_all, potential, stick_col):
    return per_device_rows(psi_block, psi_all, potential, stick_col)


def solution(mesh):
    return jax.shard_map(
        per_device,
        mesh=mesh,
        in_specs=(
            P(None, "band", "pw", None),
            P(None, "band", "pw", None),
            P("pw", None, None),
            P(),
        ),
        out_specs=(P(None, "pw", "band"), P(None, "band", "pw", None)),
        check_vma=False,
    )
```

```python
import math

import jax
import numpy as np
import jax.numpy as jnp
from jax import lax
from jax.sharding import PartitionSpec as P


def frequency(index, size):
    return jnp.where(index < size // 2, index, index - size)


def kinetic_table(columns, grid_size):
    col_x = frequency(columns // grid_size, grid_size).astype(jnp.float32)
    col_y = frequency(columns % grid_size, grid_size).astype(jnp.float32)
    along = frequency(jnp.arange(grid_size, dtype=jnp.int32), grid_size).astype(jnp.float32)
    plane = col_x * col_x + col_y * col_y
    return 4.0 * (plane[:, None] + along[None, :] * along[None, :]) / float(grid_size * grid_size)


def dft_table(grid_size, sign):
    indices = np.arange(grid_size)
    products = indices[:, None] * indices[None, :] % grid_size
    angles = 2.0 * np.pi / grid_size * products
    cosine = np.cos(angles)
    sine = sign * np.sin(angles)
    table = np.stack([np.stack([cosine, -sine]), np.stack([sine, cosine])])
    return jnp.asarray(table.astype(np.float32))


def plane_tables(stick_col, grid_size):
    grid_iota = jnp.arange(grid_size, dtype=jnp.int32)
    col_x = stick_col // grid_size
    col_y = stick_col % grid_size
    phase_angles = (
        2.0
        * math.pi
        / grid_size
        * (grid_iota[:, None] * col_x[None, :] % grid_size).astype(jnp.float32)
    )
    place_cols = (col_y[:, None] == grid_iota[None, :]).astype(jnp.float32)
    pick_cols = (grid_iota[:, None] == col_y[None, :]).astype(jnp.float32)
    return jnp.cos(phase_angles), jnp.sin(phase_angles), place_cols, pick_cols


def mult(left, right):
    return jnp.dot(left, right, precision=lax.Precision.HIGH, preferred_element_type=jnp.float32)


def plane_phase(amp, pot, tables, grid_size):
    phase_cos, phase_sin, place_cols, pick_cols = tables
    inverse = dft_table(grid_size, 1.0)
    cosine = inverse[0, 0]
    sine = inverse[1, 0]
    scaled_pot = (pot / float(grid_size**3))[None]
    val_re = amp[0][:, :, None, :]
    val_im = amp[1][:, :, None, :]
    spread_re = val_re * phase_cos - val_im * phase_sin
    spread_im = val_re * phase_sin + val_im * phase_cos
    rows_re = mult(spread_re, place_cols)
    rows_im = mult(spread_im, place_cols)
    shared = mult(rows_re + rows_im, cosine)
    wave_re = (shared - mult(rows_im, cosine + sine)) * scaled_pot
    wave_im = (shared + mult(rows_re, sine - cosine)) * scaled_pot
    shared = mult(wave_re + wave_im, cosine)
    back_re = shared - mult(wave_im, cosine - sine)
    back_im = shared - mult(wave_re, sine + cosine)
    sel_re = mult(back_re, pick_cols)
    sel_im = mult(back_im, pick_cols)
    picked_re = jnp.sum(sel_re * phase_cos + sel_im * phase_sin, axis=2)
    picked_im = jnp.sum(sel_im * phase_cos - sel_re * phase_sin, axis=2)
    return jnp.stack([picked_re, picked_im])


def intersect(lowered, psi_all, pw_count):
    turned = jnp.stack([-lowered[1], lowered[0]])
    both = jnp.concatenate([lowered, turned], axis=1)
    dims = (((2, 3), (2, 3)), ((0,), (0,)))
    width = psi_all.shape[1] // 4
    partial_value = jnp.concatenate(
        [
            jnp.sum(
                lax.dot_general(
                    both,
                    psi_all[:, k * width : (k + 1) * width],
                    dims,
                    preferred_element_type=jnp.float32,
                ),
                axis=0,
            )
            for k in range(4)
        ],
        axis=-1,
    )
    partial_value = partial_value.reshape(2, lowered.shape[1], partial_value.shape[-1])
    rows_dev = partial_value.shape[1] // pw_count
    pieces = partial_value.reshape(2, pw_count, rows_dev, partial_value.shape[-1])
    pieces = lax.all_to_all(pieces, "pw", split_axis=1, concat_axis=1, tiled=True)
    return jnp.sum(pieces, axis=1)


def per_device_rows(psi_block, psi_all, potential, stick_col):
    sticks_dev = psi_block.shape[2]
    grid_size = psi_block.shape[3]
    fast = lax.Precision.HIGH
    rank = lax.axis_index("pw")
    pw_count = lax.axis_size("pw")
    planes = potential.shape[0]
    my_columns = lax.dynamic_slice_in_dim(stick_col, rank * sticks_dev, sticks_dev)
    kinetic = kinetic_table(my_columns, grid_size)
    inverse = dft_table(grid_size, 1.0)
    forward = dft_table(grid_size, -1.0)
    tables = plane_tables(stick_col, grid_size)
    parts = []
    for band in range(psi_block.shape[1]):
        coeffs = psi_block[:, band : band + 1]
        z_lines = jnp.einsum("dczk,cbsk->zdbs", inverse, coeffs, precision=fast)
        received = lax.all_to_all(z_lines, "pw", split_axis=0, concat_axis=0, tiled=True)
        lanes = received.shape[1:]
        received = received.reshape((pw_count, planes) + lanes)
        amp = jnp.transpose(received, (2, 3, 1, 0, 4)).reshape(
            lanes[0], lanes[1], planes, pw_count * sticks_dev
        )
        picked = plane_phase(amp, potential, tables, grid_size)
        outgoing = picked.reshape(lanes[0], lanes[1], planes, pw_count, sticks_dev)
        outgoing = jnp.transpose(outgoing, (3, 2, 0, 1, 4)).reshape((pw_count * planes,) + lanes)
        sticks_back = lax.all_to_all(outgoing, "pw", split_axis=0, concat_axis=0, tiled=True)
        parts.append(jnp.einsum("dckz,zcbs->dbsk", forward, sticks_back, precision=fast))
    vpsi = jnp.concatenate(parts, axis=1)
    applied = kinetic[None, None] * psi_block + vpsi
    lowered = applied.astype(jnp.bfloat16)
    gathered = lax.all_gather(lowered, "band", axis=1, tiled=True)
    intersection = intersect(gathered, psi_all, pw_count)
    return (intersection, applied)


def per_device(psi_block, psi_all, potential, stick_col):
    return per_device_rows(psi_block, psi_all, potential, stick_col)


def solution(mesh):
    return jax.shard_map(
        per_device,
        mesh=mesh,
        in_specs=(
            P(None, "band", "pw", None),
            P(None, "band", "pw", None),
            P("pw", None, None),
            P(),
        ),
        out_specs=(P(None, "pw", "band"), P(None, "band", "pw", None)),
        check_vma=False,
    )
```

```python
import math

import jax
import numpy as np
import jax.numpy as jnp
from jax import lax
from jax.sharding import PartitionSpec as P


def frequency(index, size):
    return jnp.where(index < size // 2, index, index - size)


def kinetic_table(columns, grid_size):
    col_x = frequency(columns // grid_size, grid_size).astype(jnp.float32)
    col_y = frequency(columns % grid_size, grid_size).astype(jnp.float32)
    along = frequency(jnp.arange(grid_size, dtype=jnp.int32), grid_size).astype(jnp.float32)
    plane = col_x * col_x + col_y * col_y
    return 4.0 * (plane[:, None] + along[None, :] * along[None, :]) / float(grid_size * grid_size)


def dft_table(grid_size, sign):
    indices = np.arange(grid_size)
    products = indices[:, None] * indices[None, :] % grid_size
    angles = 2.0 * np.pi / grid_size * products
    cosine = np.cos(angles)
    sine = sign * np.sin(angles)
    table = np.stack([np.stack([cosine, -sine]), np.stack([sine, cosine])])
    return jnp.asarray(table.astype(np.float32))


def plane_tables(stick_col, grid_size):
    grid_iota = jnp.arange(grid_size, dtype=jnp.int32)
    col_x = stick_col // grid_size
    col_y = stick_col % grid_size
    phase_angles = (
        2.0
        * math.pi
        / grid_size
        * (grid_iota[:, None] * col_x[None, :] % grid_size).astype(jnp.float32)
    )
    place_cols = (col_y[:, None] == grid_iota[None, :]).astype(jnp.float32)
    pick_cols = (grid_iota[:, None] == col_y[None, :]).astype(jnp.float32)
    return jnp.cos(phase_angles), jnp.sin(phase_angles), place_cols, pick_cols


def mult(left, right):
    return jnp.dot(left, right, precision=lax.Precision.HIGH, preferred_element_type=jnp.float32)


def plane_phase(amp, pot, tables, grid_size):
    phase_cos, phase_sin, place_cols, pick_cols = tables
    inverse = dft_table(grid_size, 1.0)
    cosine = inverse[0, 0]
    sine = inverse[1, 0]
    scaled_pot = (pot / float(grid_size**3))[None]
    val_re = amp[0][:, :, None, :]
    val_im = amp[1][:, :, None, :]
    spread_re = val_re * phase_cos - val_im * phase_sin
    spread_im = val_re * phase_sin + val_im * phase_cos
    rows_re = mult(spread_re, place_cols)
    rows_im = mult(spread_im, place_cols)
    shared = mult(rows_re + rows_im, cosine)
    wave_re = (shared - mult(rows_im, cosine + sine)) * scaled_pot
    wave_im = (shared + mult(rows_re, sine - cosine)) * scaled_pot
    shared = mult(wave_re + wave_im, cosine)
    back_re = shared - mult(wave_im, cosine - sine)
    back_im = shared - mult(wave_re, sine + cosine)
    sel_re = mult(back_re, pick_cols)
    sel_im = mult(back_im, pick_cols)
    picked_re = jnp.sum(sel_re * phase_cos + sel_im * phase_sin, axis=2)
    picked_im = jnp.sum(sel_im * phase_cos - sel_re * phase_sin, axis=2)
    return jnp.stack([picked_re, picked_im])


def intersect(lowered, psi_all, pw_count):
    turned = jnp.stack([-lowered[1], lowered[0]])
    both = jnp.stack([lowered, turned], axis=2).reshape(
        (lowered.shape[0], 2 * lowered.shape[1]) + lowered.shape[2:]
    )
    dims = (((2, 3), (2, 3)), ((0,), (0,)))
    width = psi_all.shape[1] // 4
    partial_value = jnp.concatenate(
        [
            jnp.sum(
                lax.dot_general(
                    both,
                    psi_all[:, k * width : (k + 1) * width],
                    dims,
                    preferred_element_type=jnp.float32,
                ),
                axis=0,
            )
            for k in range(4)
        ],
        axis=-1,
    )
    rows_dev = lowered.shape[1] // pw_count
    pieces = partial_value.reshape(pw_count, rows_dev * 2 * partial_value.shape[-1])
    pieces = lax.all_to_all(pieces, "pw", split_axis=0, concat_axis=0, tiled=True)
    summed = jnp.sum(pieces, axis=0).reshape(rows_dev, 2, partial_value.shape[-1])
    return jnp.transpose(summed, (1, 0, 2))


def per_device_rows(psi_block, psi_all, potential, stick_col):
    sticks_dev = psi_block.shape[2]
    grid_size = psi_block.shape[3]
    fast = lax.Precision.HIGH
    rank = lax.axis_index("pw")
    pw_count = lax.axis_size("pw")
    planes = potential.shape[0]
    my_columns = lax.dynamic_slice_in_dim(stick_col, rank * sticks_dev, sticks_dev)
    kinetic = kinetic_table(my_columns, grid_size)
    inverse = dft_table(grid_size, 1.0)
    forward = dft_table(grid_size, -1.0)
    tables = plane_tables(stick_col, grid_size)
    z_lines = jnp.einsum("dczk,cbsk->zdbs", inverse, psi_block, precision=fast)
    received = lax.all_to_all(z_lines, "pw", split_axis=0, concat_axis=0, tiled=True)
    lanes = received.shape[1:]
    received = received.reshape((pw_count, planes) + lanes)
    amp = jnp.transpose(received, (2, 3, 1, 0, 4)).reshape(
        lanes[0], lanes[1], planes, pw_count * sticks_dev
    )
    picked = plane_phase(amp, potential, tables, grid_size)
    outgoing = picked.reshape(lanes[0], lanes[1], planes, pw_count, sticks_dev)
    outgoing = jnp.transpose(outgoing, (3, 2, 0, 1, 4)).reshape((pw_count * planes,) + lanes)
    sticks_back = lax.all_to_all(outgoing, "pw", split_axis=0, concat_axis=0, tiled=True)
    vpsi = jnp.einsum("dckz,zcbs->dbsk", forward, sticks_back, precision=fast)
    applied = kinetic[None, None] * psi_block + vpsi
    lowered = applied.astype(jnp.bfloat16)
    gathered = lax.all_gather(lowered, "band", axis=1, tiled=True)
    intersection = intersect(gathered, psi_all, pw_count)
    return (intersection, applied)


def per_device(psi_block, psi_all, potential, stick_col):
    return per_device_rows(psi_block, psi_all, potential, stick_col)


def solution(mesh):
    return jax.shard_map(
        per_device,
        mesh=mesh,
        in_specs=(
            P(None, "band", "pw", None),
            P(None, "band", "pw", None),
            P("pw", None, None),
            P(),
        ),
        out_specs=(P(None, "pw", "band"), P(None, "band", "pw", None)),
        check_vma=False,
    )
```

```python
import math

import jax
import numpy as np
import jax.numpy as jnp
from jax import lax
from jax.sharding import PartitionSpec as P


def frequency(index, size):
    return jnp.where(index < size // 2, index, index - size)


def kinetic_table(columns, grid_size):
    col_x = frequency(columns // grid_size, grid_size).astype(jnp.float32)
    col_y = frequency(columns % grid_size, grid_size).astype(jnp.float32)
    along = frequency(jnp.arange(grid_size, dtype=jnp.int32), grid_size).astype(jnp.float32)
    plane = col_x * col_x + col_y * col_y
    return 4.0 * (plane[:, None] + along[None, :] * along[None, :]) / float(grid_size * grid_size)


def dft_table(grid_size, sign):
    indices = np.arange(grid_size)
    products = indices[:, None] * indices[None, :] % grid_size
    angles = 2.0 * np.pi / grid_size * products
    cosine = np.cos(angles)
    sine = sign * np.sin(angles)
    table = np.stack([np.stack([cosine, -sine]), np.stack([sine, cosine])])
    return jnp.asarray(table.astype(np.float32))


def plane_tables(stick_col, grid_size):
    grid_iota = jnp.arange(grid_size, dtype=jnp.int32)
    col_x = stick_col // grid_size
    col_y = stick_col % grid_size
    phase_angles = (
        2.0
        * math.pi
        / grid_size
        * (grid_iota[:, None] * col_x[None, :] % grid_size).astype(jnp.float32)
    )
    place_cols = (col_y[:, None] == grid_iota[None, :]).astype(jnp.float32)
    pick_cols = (grid_iota[:, None] == col_y[None, :]).astype(jnp.float32)
    return jnp.cos(phase_angles), jnp.sin(phase_angles), place_cols, pick_cols


def mult(left, right):
    return jnp.dot(left, right, precision=lax.Precision.HIGH, preferred_element_type=jnp.float32)


def plane_phase(amp, pot, tables, grid_size):
    phase_cos, phase_sin, place_cols, pick_cols = tables
    inverse = dft_table(grid_size, 1.0)
    cosine = inverse[0, 0]
    sine = inverse[1, 0]
    scaled_pot = (pot / float(grid_size**3))[None]
    val_re = amp[0][:, :, None, :]
    val_im = amp[1][:, :, None, :]
    spread_re = val_re * phase_cos - val_im * phase_sin
    spread_im = val_re * phase_sin + val_im * phase_cos
    rows_re = mult(spread_re, place_cols)
    rows_im = mult(spread_im, place_cols)
    shared = mult(rows_re + rows_im, cosine)
    wave_re = (shared - mult(rows_im, cosine + sine)) * scaled_pot
    wave_im = (shared + mult(rows_re, sine - cosine)) * scaled_pot
    shared = mult(wave_re + wave_im, cosine)
    back_re = shared - mult(wave_im, cosine - sine)
    back_im = shared - mult(wave_re, sine + cosine)
    sel_re = mult(back_re, pick_cols)
    sel_im = mult(back_im, pick_cols)
    picked_re = jnp.sum(sel_re * phase_cos + sel_im * phase_sin, axis=2)
    picked_im = jnp.sum(sel_im * phase_cos - sel_re * phase_sin, axis=2)
    return jnp.stack([picked_re, picked_im])


def intersect(lowered, psi_all, pw_count):
    turned = jnp.stack([-lowered[1], lowered[0]])
    both = jnp.stack([lowered, turned], axis=2).reshape(
        (lowered.shape[0], 2 * lowered.shape[1]) + lowered.shape[2:]
    )
    dims = (((2, 3), (2, 3)), ((0,), (0,)))
    width = psi_all.shape[1] // 4
    partial_value = jnp.concatenate(
        [
            jnp.sum(
                lax.dot_general(
                    both,
                    psi_all[:, k * width : (k + 1) * width],
                    dims,
                    preferred_element_type=jnp.float32,
                ),
                axis=0,
            )
            for k in range(4)
        ],
        axis=-1,
    )
    rows_dev = lowered.shape[1] // pw_count
    pieces = partial_value.reshape(pw_count, rows_dev * 2 * partial_value.shape[-1])
    pieces = lax.all_to_all(pieces, "pw", split_axis=0, concat_axis=0, tiled=True)
    summed = jnp.sum(pieces, axis=0).reshape(rows_dev, 2, partial_value.shape[-1])
    return jnp.transpose(summed, (1, 0, 2))


def per_device_rows(psi_block, psi_all, potential, stick_col):
    sticks_dev = psi_block.shape[2]
    grid_size = psi_block.shape[3]
    fast = lax.Precision.HIGH
    rank = lax.axis_index("pw")
    pw_count = lax.axis_size("pw")
    planes = potential.shape[0]
    my_columns = lax.dynamic_slice_in_dim(stick_col, rank * sticks_dev, sticks_dev)
    kinetic = kinetic_table(my_columns, grid_size)
    inverse = dft_table(grid_size, 1.0)
    forward = dft_table(grid_size, -1.0)
    tables = plane_tables(stick_col, grid_size)
    z_lines = jnp.einsum("dczk,cbsk->zdbs", inverse, psi_block, precision=fast)
    lanes = z_lines.shape[1:]
    received = lax.all_to_all(
        z_lines.reshape(pw_count, -1), "pw", split_axis=0, concat_axis=0, tiled=True
    )
    received = received.reshape((pw_count, planes) + lanes)
    amp = jnp.transpose(received, (2, 3, 1, 0, 4)).reshape(
        lanes[0], lanes[1], planes, pw_count * sticks_dev
    )
    picked = plane_phase(amp, potential, tables, grid_size)
    outgoing = picked.reshape(lanes[0], lanes[1], planes, pw_count, sticks_dev)
    outgoing = jnp.transpose(outgoing, (3, 2, 0, 1, 4)).reshape(pw_count, -1)
    sticks_back = lax.all_to_all(outgoing, "pw", split_axis=0, concat_axis=0, tiled=True)
    sticks_back = sticks_back.reshape((pw_count * planes,) + lanes)
    vpsi = jnp.einsum("dckz,zcbs->dbsk", forward, sticks_back, precision=fast)
    applied = kinetic[None, None] * psi_block + vpsi
    lowered = applied.astype(jnp.bfloat16)
    gathered = lax.all_gather(lowered, "band", axis=1, tiled=True)
    intersection = intersect(gathered, psi_all, pw_count)
    return (intersection, applied)


def per_device(psi_block, psi_all, potential, stick_col):
    return per_device_rows(psi_block, psi_all, potential, stick_col)


def solution(mesh):
    return jax.shard_map(
        per_device,
        mesh=mesh,
        in_specs=(
            P(None, "band", "pw", None),
            P(None, "band", "pw", None),
            P("pw", None, None),
            P(),
        ),
        out_specs=(P(None, "pw", "band"), P(None, "band", "pw", None)),
        check_vma=False,
    )
```

```python
import math

import jax
import numpy as np
import jax.numpy as jnp
from jax import lax
from jax.sharding import PartitionSpec as P


def frequency(index, size):
    return jnp.where(index < size // 2, index, index - size)


def kinetic_table(columns, grid_size):
    col_x = frequency(columns // grid_size, grid_size).astype(jnp.float32)
    col_y = frequency(columns % grid_size, grid_size).astype(jnp.float32)
    along = frequency(jnp.arange(grid_size, dtype=jnp.int32), grid_size).astype(jnp.float32)
    plane = col_x * col_x + col_y * col_y
    return 4.0 * (plane[:, None] + along[None, :] * along[None, :]) / float(grid_size * grid_size)


def dft_table(grid_size, sign):
    indices = np.arange(grid_size)
    products = indices[:, None] * indices[None, :] % grid_size
    angles = 2.0 * np.pi / grid_size * products
    cosine = np.cos(angles)
    sine = sign * np.sin(angles)
    table = np.stack([np.stack([cosine, -sine]), np.stack([sine, cosine])])
    return jnp.asarray(table.astype(np.float32))


def plane_tables(stick_col, grid_size):
    grid_iota = jnp.arange(grid_size, dtype=jnp.int32)
    col_x = stick_col // grid_size
    col_y = stick_col % grid_size
    phase_angles = (
        2.0
        * math.pi
        / grid_size
        * (grid_iota[:, None] * col_x[None, :] % grid_size).astype(jnp.float32)
    )
    place_cols = (col_y[:, None] == grid_iota[None, :]).astype(jnp.float32)
    pick_cols = (grid_iota[:, None] == col_y[None, :]).astype(jnp.float32)
    return jnp.cos(phase_angles), jnp.sin(phase_angles), place_cols, pick_cols


def mult(left, right):
    return jnp.dot(left, right, precision=lax.Precision.HIGH, preferred_element_type=jnp.float32)


def plane_phase(amp, pot, tables, grid_size):
    phase_cos, phase_sin, place_cols, pick_cols = tables
    inverse = dft_table(grid_size, 1.0)
    cosine = inverse[0, 0]
    sine = inverse[1, 0]
    scaled_pot = (pot / float(grid_size**3))[None]
    val_re = amp[0][:, :, None, :]
    val_im = amp[1][:, :, None, :]
    spread_re = val_re * phase_cos - val_im * phase_sin
    spread_im = val_re * phase_sin + val_im * phase_cos
    rows_re = mult(spread_re, place_cols)
    rows_im = mult(spread_im, place_cols)
    shared = mult(rows_re + rows_im, cosine)
    wave_re = (shared - mult(rows_im, cosine + sine)) * scaled_pot
    wave_im = (shared + mult(rows_re, sine - cosine)) * scaled_pot
    shared = mult(wave_re + wave_im, cosine)
    back_re = shared - mult(wave_im, cosine - sine)
    back_im = shared - mult(wave_re, sine + cosine)
    sel_re = mult(back_re, pick_cols)
    sel_im = mult(back_im, pick_cols)
    picked_re = jnp.sum(sel_re * phase_cos + sel_im * phase_sin, axis=2)
    picked_im = jnp.sum(sel_im * phase_cos - sel_re * phase_sin, axis=2)
    return jnp.stack([picked_re, picked_im])


def intersect(lowered, psi_all, pw_count):
    turned = jnp.stack([-lowered[1], lowered[0]])
    both = jnp.stack([lowered, turned], axis=2).reshape(
        (lowered.shape[0], 2 * lowered.shape[1]) + lowered.shape[2:]
    )
    dims = (((2, 3), (2, 3)), ((0,), (0,)))
    width = psi_all.shape[1] // 4
    partial_value = jnp.concatenate(
        [
            jnp.sum(
                lax.dot_general(
                    both,
                    psi_all[:, k * width : (k + 1) * width],
                    dims,
                    preferred_element_type=jnp.float32,
                ),
                axis=0,
            )
            for k in range(4)
        ],
        axis=-1,
    )
    rows_dev = lowered.shape[1] // pw_count
    pieces = partial_value.reshape(pw_count, rows_dev * 2 * partial_value.shape[-1])
    pieces = lax.all_to_all(pieces, "pw", split_axis=0, concat_axis=0, tiled=True)
    summed = jnp.sum(pieces, axis=0).reshape(rows_dev, 2, partial_value.shape[-1])
    return jnp.transpose(summed, (1, 0, 2))


def per_device_rows(psi_block, psi_all, potential, stick_col):
    sticks_dev = psi_block.shape[2]
    grid_size = psi_block.shape[3]
    fast = lax.Precision.HIGH
    rank = lax.axis_index("pw")
    pw_count = lax.axis_size("pw")
    planes = potential.shape[0]
    my_columns = lax.dynamic_slice_in_dim(stick_col, rank * sticks_dev, sticks_dev)
    kinetic = kinetic_table(my_columns, grid_size)
    inverse = dft_table(grid_size, 1.0)
    forward = dft_table(grid_size, -1.0)
    tables = plane_tables(stick_col, grid_size)
    inverse_split = inverse.reshape(2, 2, pw_count, planes, grid_size)
    z_lines = jnp.einsum("dcpzk,cbsk->pdbzs", inverse_split, psi_block, precision=fast)
    lanes = z_lines.shape[1:3]
    received = lax.all_to_all(
        z_lines.reshape(pw_count, -1), "pw", split_axis=0, concat_axis=0, tiled=True
    )
    received = received.reshape((pw_count,) + lanes + (planes, sticks_dev))
    amp = jnp.transpose(received, (1, 2, 3, 0, 4)).reshape(
        lanes[0], lanes[1], planes, pw_count * sticks_dev
    )
    picked = plane_phase(amp, potential, tables, grid_size)
    outgoing = picked.reshape(lanes[0], lanes[1], planes, pw_count, sticks_dev)
    outgoing = jnp.transpose(outgoing, (3, 2, 0, 1, 4)).reshape(pw_count, -1)
    sticks_back = lax.all_to_all(outgoing, "pw", split_axis=0, concat_axis=0, tiled=True)
    sticks_back = sticks_back.reshape((pw_count * planes,) + lanes + (sticks_dev,))
    vpsi = jnp.einsum("dckz,zcbs->dbsk", forward, sticks_back, precision=fast)
    applied = kinetic[None, None] * psi_block + vpsi
    lowered = applied.astype(jnp.bfloat16)
    gathered = lax.all_gather(lowered, "band", axis=1, tiled=True)
    intersection = intersect(gathered, psi_all, pw_count)
    return (intersection, applied)


def per_device(psi_block, psi_all, potential, stick_col):
    return per_device_rows(psi_block, psi_all, potential, stick_col)


def solution(mesh):
    return jax.shard_map(
        per_device,
        mesh=mesh,
        in_specs=(
            P(None, "band", "pw", None),
            P(None, "band", "pw", None),
            P("pw", None, None),
            P(),
        ),
        out_specs=(P(None, "pw", "band"), P(None, "band", "pw", None)),
        check_vma=False,
    )
```

```python
import math

import jax
import numpy as np
import jax.numpy as jnp
from jax import lax
from jax.sharding import PartitionSpec as P


def frequency(index, size):
    return jnp.where(index < size // 2, index, index - size)


def kinetic_table(columns, grid_size):
    col_x = frequency(columns // grid_size, grid_size).astype(jnp.float32)
    col_y = frequency(columns % grid_size, grid_size).astype(jnp.float32)
    along = frequency(jnp.arange(grid_size, dtype=jnp.int32), grid_size).astype(jnp.float32)
    plane = col_x * col_x + col_y * col_y
    return 4.0 * (plane[:, None] + along[None, :] * along[None, :]) / float(grid_size * grid_size)


def dft_table(grid_size, sign):
    indices = np.arange(grid_size)
    products = indices[:, None] * indices[None, :] % grid_size
    angles = 2.0 * np.pi / grid_size * products
    cosine = np.cos(angles)
    sine = sign * np.sin(angles)
    table = np.stack([np.stack([cosine, -sine]), np.stack([sine, cosine])])
    return jnp.asarray(table.astype(np.float32))


def plane_tables(stick_col, grid_size):
    grid_iota = jnp.arange(grid_size, dtype=jnp.int32)
    col_x = stick_col // grid_size
    col_y = stick_col % grid_size
    phase_angles = (
        2.0
        * math.pi
        / grid_size
        * (grid_iota[:, None] * col_x[None, :] % grid_size).astype(jnp.float32)
    )
    place_cols = (col_y[:, None] == grid_iota[None, :]).astype(jnp.float32)
    pick_cols = (grid_iota[:, None] == col_y[None, :]).astype(jnp.float32)
    return jnp.cos(phase_angles), jnp.sin(phase_angles), place_cols, pick_cols


def mult(left, right):
    return jnp.dot(left, right, precision=lax.Precision.HIGH, preferred_element_type=jnp.float32)


def plane_phase(amp, pot, tables, grid_size):
    phase_cos, phase_sin, place_cols, pick_cols = tables
    inverse = dft_table(grid_size, 1.0)
    cosine = inverse[0, 0]
    sine = inverse[1, 0]
    scaled_pot = (pot / float(grid_size**3))[None]
    val_re = amp[0][:, :, None, :]
    val_im = amp[1][:, :, None, :]
    spread_re = val_re * phase_cos - val_im * phase_sin
    spread_im = val_re * phase_sin + val_im * phase_cos
    rows_re = mult(spread_re, place_cols)
    rows_im = mult(spread_im, place_cols)
    shared = mult(rows_re + rows_im, cosine)
    wave_re = (shared - mult(rows_im, cosine + sine)) * scaled_pot
    wave_im = (shared + mult(rows_re, sine - cosine)) * scaled_pot
    shared = mult(wave_re + wave_im, cosine)
    back_re = shared - mult(wave_im, cosine - sine)
    back_im = shared - mult(wave_re, sine + cosine)
    sel_re = mult(back_re, pick_cols)
    sel_im = mult(back_im, pick_cols)
    picked_re = jnp.sum(sel_re * phase_cos + sel_im * phase_sin, axis=2)
    picked_im = jnp.sum(sel_im * phase_cos - sel_re * phase_sin, axis=2)
    return jnp.stack([picked_re, picked_im])


def intersect(lowered, psi_all, pw_count):
    turned = jnp.stack([-lowered[1], lowered[0]])
    both = jnp.stack([lowered, turned], axis=2).reshape(
        (lowered.shape[0], 2 * lowered.shape[1]) + lowered.shape[2:]
    )
    dims = (((2, 3), (2, 3)), ((0,), (0,)))
    width = psi_all.shape[1] // 4
    partial_value = jnp.concatenate(
        [
            jnp.sum(
                lax.dot_general(
                    both,
                    psi_all[:, k * width : (k + 1) * width],
                    dims,
                    preferred_element_type=jnp.float32,
                ),
                axis=0,
            )
            for k in range(4)
        ],
        axis=-1,
    )
    rows_dev = lowered.shape[1] // pw_count
    pieces = partial_value.reshape(pw_count, rows_dev * 2 * partial_value.shape[-1])
    pieces = lax.all_to_all(pieces, "pw", split_axis=0, concat_axis=0, tiled=True)
    summed = jnp.sum(pieces, axis=0).reshape(rows_dev, 2, partial_value.shape[-1])
    return jnp.transpose(summed, (1, 0, 2))


def per_device_rows(psi_block, psi_all, potential, stick_col):
    sticks_dev = psi_block.shape[2]
    grid_size = psi_block.shape[3]
    fast = lax.Precision.HIGH
    rank = lax.axis_index("pw")
    pw_count = lax.axis_size("pw")
    planes = potential.shape[0]
    my_columns = lax.dynamic_slice_in_dim(stick_col, rank * sticks_dev, sticks_dev)
    kinetic = kinetic_table(my_columns, grid_size)
    inverse = dft_table(grid_size, 1.0)
    forward = dft_table(grid_size, -1.0)
    tables = plane_tables(stick_col, grid_size)
    inverse_split = inverse.reshape(2, 2, pw_count, planes, grid_size)
    z_lines = jnp.einsum("dcpzk,cbsk->pdbzs", inverse_split, psi_block, precision=fast)
    lanes = z_lines.shape[1:3]
    received = lax.all_to_all(
        z_lines.reshape(pw_count, -1), "pw", split_axis=0, concat_axis=0, tiled=True
    )
    received = received.reshape((pw_count,) + lanes + (planes, sticks_dev))
    amp = jnp.transpose(received, (1, 2, 3, 0, 4)).reshape(
        lanes[0], lanes[1], planes, pw_count * sticks_dev
    )
    picked = plane_phase(amp, potential, tables, grid_size)
    outgoing = picked.reshape(lanes[0], lanes[1], planes, pw_count, sticks_dev)
    outgoing = jnp.transpose(outgoing, (3, 0, 1, 2, 4)).reshape(pw_count, -1)
    sticks_back = lax.all_to_all(outgoing, "pw", split_axis=0, concat_axis=0, tiled=True)
    sticks_back = sticks_back.reshape((pw_count,) + lanes + (planes, sticks_dev))
    forward_split = forward.reshape(2, 2, grid_size, pw_count, planes)
    vpsi = jnp.einsum("dckpz,pcbzs->dbsk", forward_split, sticks_back, precision=fast)
    applied = kinetic[None, None] * psi_block + vpsi
    lowered = applied.astype(jnp.bfloat16)
    gathered = lax.all_gather(lowered, "band", axis=1, tiled=True)
    intersection = intersect(gathered, psi_all, pw_count)
    return (intersection, applied)


def per_device(psi_block, psi_all, potential, stick_col):
    return per_device_rows(psi_block, psi_all, potential, stick_col)


def solution(mesh):
    return jax.shard_map(
        per_device,
        mesh=mesh,
        in_specs=(
            P(None, "band", "pw", None),
            P(None, "band", "pw", None),
            P("pw", None, None),
            P(),
        ),
        out_specs=(P(None, "pw", "band"), P(None, "band", "pw", None)),
        check_vma=False,
    )
```
